512 devices in a mesh: tile: 64 (over z, x_hi, core), chan: 8 (over x_lo, y).
Axes of the slice: x: 4 (x_hi: 2, x_lo: 2; x = x_hi * 2 + x_lo), y: 4, z: 16, core: 2. Of those that a mesh axis runs over, the one named last changes fastest.
Arguments:
- analysis: bfloat16 [64, 524288], P('chan', 'tile'), may hold values from -6 to 6
- send_rows: int32 [64, 5, 128], P('tile'), may hold values from 0 to 8191
- send_count: int32 [64, 5], P('tile'), may hold values from 64 to 128, as said below
- corner_slot: int32 [4, 2048, 256], P(None, 'tile'), may hold values from 0 to 639, as said below
- corner_weight: float32 [4, 2048, 256], P(None, 'tile'), may hold values from 0.1 to 0.6
- beside: int32 [2048, 8], P('tile'), may hold values from 0 to 2047, as said below
- quarter_turns: int32 [2048, 8], P('tile'), may hold values from 0 to 3
- kernel_one: bfloat16 [9, 128, 64], P(None, 'chan'), may hold values from -0.375 to 0.375
- kernel_two: bfloat16 [9, 128, 128], P(None, 'chan'), may hold values from -0.25 to 0.25
- kernel_three: bfloat16 [9, 128, 128], P(None, 'chan'), may hold values from -0.25 to 0.25
Outputs:
- forecast: bfloat16 [128, 2048, 256], P('chan', 'tile')
The draws below stay inside these ranges and needn't reach their ends.
Inputs may be any that keep to these rules, and one draw needn't show every extreme that they name: send_count[s, d] is at least 64; every shard sends 128 to itself (d = 2), and some receiver gets 128 from each of its 5 senders. corner_slot[j, t, i] = d * 128 + k names a live slot, k < send_count[s, d], of the block that shard s = (e - d + 2) mod the shard count sends to the shard e holding tile t; the four corners of a pixel are slots k, k + 1, k + 2, k + 3 of one block. beside[t, k] = (t + d) mod 2048 with 1 <= |d| <= 2.
All inputs are finite; a program needn't handle non-finite values.
Results may differ from the reference program's by a relative error of at most 0.007.
Values may be sent and summed in bfloat16 or wider, within the bound.
No kernel may reach another device: no remote copies, remote signals or barrier semaphores. Data moves between devices by JAX's collectives and lax.ppermute only.
A program may use at most 64 MiB of HBM per device.

```python
import jax
import jax.numpy as jnp
import numpy as np
from jax import lax

CIN = 64
COUT = 128
P_SIZE = 16
PP = 256
TILE_DEV = 32
TILES = 2048
LL_DEV = 8192
LL = 524288
CAP = 128
REACH = 2
NEAR = 5
N_TILE = 64


def receive_loads(key):
    shards = TILES // TILE_DEV
    near_count = 2 * REACH + 1
    folded = jax.random.fold_in(key, 71)
    counts = jax.random.randint(jax.random.fold_in(folded, 2), (shards, near_count), CAP // 2, CAP + 1)
    full_one = jax.random.randint(jax.random.fold_in(folded, 3), (), 0, shards)
    row_ids = jnp.arange(shards)[:, None]
    col_ids = jnp.arange(near_count)[None, :]
    counts = jnp.where(row_ids == full_one, CAP, counts)
    counts = jnp.where(col_ids == REACH, CAP, counts)
    return counts.astype(jnp.int32)


def draw_send_count(key, part):
    shards = TILES // TILE_DEV
    near_count = 2 * REACH + 1
    received = receive_loads(key)
    target = jnp.remainder(jnp.arange(shards)[:, None] + jnp.arange(near_count)[None, :] - REACH, shards)
    return received[target, jnp.arange(near_count)[None, :]].astype(jnp.int32)


def draw_corner_slot(key, part):
    shards = TILES // TILE_DEV
    received = receive_loads(key)
    upper_edge = jnp.cumsum(received, axis=1)
    lower_edge = upper_edge - received
    totals = upper_edge[:, -1]
    span = TILE_DEV * PP
    picked = jax.random.randint(jax.random.fold_in(key, 5), (shards, span), 0, totals[:, None])
    position = jnp.arange(span)[None, :]
    picked = jnp.where(position == 0, totals[:, None] - 1, picked)
    picked = jnp.where(position == 1, 0, picked)
    block = jnp.sum((picked[:, :, None] >= upper_edge[:, None, :]).astype(jnp.int32), axis=2)
    low_start = jnp.take_along_axis(lower_edge, block, axis=1)
    block_count = jnp.take_along_axis(received, block, axis=1)
    first_slot = jnp.minimum(picked - low_start, block_count - 4)
    corners = jnp.stack([block * CAP + first_slot + j for j in range(4)], axis=0)
    return corners.reshape(4, TILES, PP).astype(jnp.int32)


def draw_beside(key, part):
    steps_away = jax.random.randint(jax.random.fold_in(key, 31), (TILES, 8), 1, REACH + 1)
    flipped = jax.random.randint(jax.random.fold_in(key, 32), (TILES, 8), 0, 2)
    offset = jnp.where(flipped == 1, -steps_away, steps_away)
    offset = offset.at[0, 2].set(-1).at[TILES - 1, 3].set(1)
    return jnp.remainder(jnp.arange(TILES)[:, None] + offset, TILES).astype(jnp.int32)


def place_ends(values, rng, low, high):
    dims = values.shape
    index_at = [jax.random.randint(jax.random.fold_in(rng, axis), (), 0, dims[axis]) for axis in range(len(dims))]
    values = values.at[tuple(index_at)].set(low)
    longest = dims.index(max(dims))
    index_at[longest] = (index_at[longest] + 1) % dims[longest]
    return values.at[tuple(index_at)].set(high)


def block_levels(rng, shape, cuts, smallest, high):
    gain = 1.0
    for dim, shards_of in cuts:
        heights = jax.random.uniform(jax.random.fold_in(jax.random.fold_in(rng, 6), dim), (shards_of,), jnp.float32, smallest / len(cuts), high / len(cuts))
        gain = gain * jnp.repeat(jnp.exp(heights), shape[dim] // shards_of).reshape((-1,) + (1,) * (len(shape) - 1 - dim))
    return gain


def gaussian(rng, shape, width, bound, pieces=(), held_as=jnp.bfloat16):
    values = jax.random.normal(rng, shape, jnp.float32) * width
    if len(pieces) > 0:
        values = block_levels(rng, shape, pieces, -0.22, 0.18) * values
    return jnp.clip(values, min=-bound, max=bound).astype(held_as)


def setup_inputs(seed: int = 0) -> dict:
    streams_of = jax.random.split(jax.random.key(seed), 11)
    return {
        "analysis": gaussian(streams_of[0], (CIN, LL), 1.0, 6.0, ((0, 8), (1, 64))),
        "send_rows": place_ends(jax.random.randint(streams_of[1], (N_TILE, NEAR, CAP), 0, LL_DEV), jax.random.fold_in(streams_of[1], 1), 0, LL_DEV - 1).astype(jnp.int32),
        "send_count": draw_send_count(jax.random.fold_in(streams_of[10], 71), 0),
        "corner_slot": draw_corner_slot(jax.random.fold_in(streams_of[10], 71), 0),
        "corner_weight": jnp.clip(0.1 + 0.5 * jax.random.uniform(streams_of[4], (4, TILES, PP), jnp.float32) ** block_levels(streams_of[4], (4, TILES, PP), ((1, 64),), -0.2, 0.2), 0.1, 0.6),
        "beside": draw_beside(jax.random.fold_in(streams_of[10], 71), 0),
        "quarter_turns": place_ends(jax.random.randint(streams_of[6], (TILES, 8), 0, 4), jax.random.fold_in(streams_of[6], 1), 0, 3).astype(jnp.int32),
        "kernel_one": gaussian(streams_of[7], (9, COUT, CIN), (9 * CIN // 2) ** -0.5, 0.375, ((1, 8),)),
        "kernel_two": gaussian(streams_of[8], (9, COUT, COUT), (9 * COUT // 2) ** -0.5, 0.25, ((1, 8),)),
        "kernel_three": gaussian(streams_of[9], (9, COUT, COUT), (9 * COUT // 2) ** -0.5, 0.25, ((1, 8),)),
    }


def cycle_table(extent):
    length = 4 * extent - 4
    entries = []
    for cycle_pos in range(length):
        if cycle_pos < extent:
            row_at, col_at = cycle_pos, 0
        elif cycle_pos < 2 * extent - 1:
            row_at, col_at = extent - 1, cycle_pos - extent + 1
        elif cycle_pos < 3 * extent - 2:
            row_at, col_at = 3 * extent - 3 - cycle_pos, extent - 1
        else:
            row_at, col_at = 0, 4 * extent - 4 - cycle_pos
        entries.append(row_at * extent + col_at)
    return np.array(entries, np.int32)


def border_tables(extent):
    length = 4 * extent - 4
    heading = []
    anchor = []
    for col_at in range(extent):
        heading.append(0)
        anchor.append(extent - 1 + col_at)
    for col_at in range(extent):
        heading.append(1)
        anchor.append((length - col_at) % length)
    for row_at in range(extent):
        heading.append(2)
        anchor.append(3 * extent - 3 - row_at)
    for row_at in range(extent):
        heading.append(3)
        anchor.append(row_at)
    heading += [4, 5, 6, 7]
    anchor += [2 * extent - 2, extent - 1, 3 * extent - 3, 0]
    return np.array(heading, np.int32), np.array(anchor, np.int32)


def layout_table(extent):
    padded_side = extent + 2
    interior = extent * extent
    entries = []
    for row_at in range(padded_side):
        for col_at in range(padded_side):
            if 1 <= row_at <= extent and 1 <= col_at <= extent:
                entries.append((row_at - 1) * extent + col_at - 1)
            elif row_at == 0 and 1 <= col_at <= extent:
                entries.append(interior + col_at - 1)
            elif row_at == padded_side - 1 and 1 <= col_at <= extent:
                entries.append(interior + extent + col_at - 1)
            elif col_at == 0 and 1 <= row_at <= extent:
                entries.append(interior + 2 * extent + row_at - 1)
            elif col_at == padded_side - 1 and 1 <= row_at <= extent:
                entries.append(interior + 3 * extent + row_at - 1)
            else:
                corner = (0 if row_at == 0 else 2) + (0 if col_at == 0 else 1)
                entries.append(interior + 4 * extent + corner)
    return np.array(entries, np.int32)


def border_values(cycle_vals, neighbours, rotations):
    heading, anchor = border_tables(P_SIZE)
    length = 4 * P_SIZE - 4
    near_tile = jnp.take(neighbours, heading, axis=1)
    near_turn = jnp.take(rotations, heading, axis=1)
    source = near_tile * length + jnp.remainder(anchor[None, :] - near_turn * (P_SIZE - 1), length)
    flat_cycles = cycle_vals.reshape(cycle_vals.shape[0], -1)
    picked = jnp.take(flat_cycles, source.reshape(-1), axis=1)
    return picked.reshape(cycle_vals.shape[0], neighbours.shape[0], 4 * P_SIZE + 4)


def stencil(padded, kernel):
    padded_side = P_SIZE + 2
    stretch = P_SIZE * padded_side - 2
    summed = jnp.zeros((kernel.shape[1], padded.shape[1], stretch), jnp.float32)
    for tap_index in range(9):
        offset = padded_side + 1 + (tap_index // 3 - 1) * padded_side + (tap_index % 3 - 1)
        window = padded[:, :, offset:offset + stretch].astype(jnp.float32)
        summed = summed + jnp.einsum('oc,ctq->otq', kernel[tap_index].astype(jnp.float32), window)
    summed = jnp.pad(summed, ((0, 0), (0, 0), (0, 2)))
    summed = summed.reshape(summed.shape[0], summed.shape[1], P_SIZE, padded_side)[:, :, :, :P_SIZE]
    summed = summed.reshape(summed.shape[0], summed.shape[1], P_SIZE * P_SIZE)
    return jax.nn.gelu(summed, approximate=False).astype(jnp.bfloat16)


def conv_all(activity, kernel, beside, quarter_turns):
    cycle_vals = jnp.take(activity, cycle_table(P_SIZE), axis=2)
    border = border_values(cycle_vals, beside, quarter_turns)
    joined = jnp.concatenate([activity, border], axis=2)
    padded = jnp.take(joined, layout_table(P_SIZE), axis=2)
    blocks = padded.reshape(padded.shape[0], TILES // TILE_DEV, TILE_DEV, padded.shape[2])
    blocks = jnp.transpose(blocks, (1, 0, 2, 3))
    result = lax.map(lambda block: stencil(block, kernel), blocks)
    return jnp.transpose(result, (1, 0, 2, 3)).reshape(kernel.shape[1], TILES, PP)


def reference(analysis, send_rows, send_count, corner_slot, corner_weight, beside, quarter_turns, kernel_one, kernel_two, kernel_three):
    shards = TILES // TILE_DEV
    slot_blocks = corner_slot.reshape(4, shards, TILE_DEV * PP)
    weight_blocks = corner_weight.reshape(4, shards, TILE_DEV * PP)

    def one_shard(receiver):
        slot_ids = jnp.take(slot_blocks, receiver, axis=1)
        weights = jnp.take(weight_blocks, receiver, axis=1)
        offset_index = slot_ids // CAP
        slot_index = slot_ids % CAP
        source = jnp.remainder(receiver - offset_index + REACH, shards).astype(jnp.int32)
        rows_sent = send_rows[source, offset_index, slot_index]
        is_live = slot_index < send_count[source, offset_index]
        point_index = (source * LL_DEV + rows_sent).astype(jnp.int32)
        values = jnp.take(analysis, point_index.reshape(-1), axis=1).reshape(CIN, 4, TILE_DEV * PP)
        values = jnp.where(is_live[None], values.astype(jnp.float32), jnp.float32(0.0))
        return jnp.sum(values * weights[None], axis=1).astype(jnp.bfloat16)

    receivers = jnp.arange(shards).astype(jnp.int32)
    regridded = lax.map(one_shard, receivers)
    regridded = jnp.transpose(regridded, (1, 0, 2)).reshape(CIN, TILES, PP)
    first = conv_all(regridded, kernel_one, beside, quarter_turns)
    second = conv_all(first, kernel_two, beside, quarter_turns)
    return conv_all(second, kernel_three, beside, quarter_turns)
```

```python
import jax
import jax.numpy as jnp
import numpy as np
from jax import lax
from jax.sharding import PartitionSpec as P

P_SIZE = 16
REACH = 2


def from_behind(value, axis, steps):
    count = lax.axis_size(axis)
    pairs = [(source, (source + steps) % count) for source in range(count)]
    return lax.ppermute(value, axis, pairs)


def extended_2(x, sides, width):
    for axis, dim in sides:
        size, length = (lax.axis_size(axis), x.shape[dim])
        up = [(i, (i + 1) % size) for i in range(size)]
        down = [(j, i) for i, j in up]
        last = lax.slice_in_dim(x, length - width, length, axis=dim)
        initial = lax.slice_in_dim(x, 0, width, axis=dim)
        before = lax.ppermute(last, axis, up)
        after = lax.ppermute(initial, axis, down)
        x = jnp.concatenate([before, x, after], axis=dim)
    return x


def cycle_table(extent):
    length = 4 * extent - 4
    entries = []
    for cycle_pos in range(length):
        if cycle_pos < extent:
            row_at, col_at = (cycle_pos, 0)
        elif cycle_pos < 2 * extent - 1:
            row_at, col_at = (extent - 1, cycle_pos - extent + 1)
        elif cycle_pos < 3 * extent - 2:
            row_at, col_at = (3 * extent - 3 - cycle_pos, extent - 1)
        else:
            row_at, col_at = (0, 4 * extent - 4 - cycle_pos)
        entries.append(row_at * extent + col_at)
    return np.array(entries, np.int32)


def border_tables(extent):
    length = 4 * extent - 4
    heading = []
    anchor = []
    for col_at in range(extent):
        heading.append(0)
        anchor.append(extent - 1 + col_at)
    for col_at in range(extent):
        heading.append(1)
        anchor.append((length - col_at) % length)
    for row_at in range(extent):
        heading.append(2)
        anchor.append(3 * extent - 3 - row_at)
    for row_at in range(extent):
        heading.append(3)
        anchor.append(row_at)
    heading += [4, 5, 6, 7]
    anchor += [2 * extent - 2, extent - 1, 3 * extent - 3, 0]
    return (np.array(heading, np.int32), np.array(anchor, np.int32))


def layout_table(extent):
    padded_side = extent + 2
    interior = extent * extent
    entries = []
    for row_at in range(padded_side):
        for col_at in range(padded_side):
            if 1 <= row_at <= extent and 1 <= col_at <= extent:
                entries.append((row_at - 1) * extent + col_at - 1)
            elif row_at == 0 and 1 <= col_at <= extent:
                entries.append(interior + col_at - 1)
            elif row_at == padded_side - 1 and 1 <= col_at <= extent:
                entries.append(interior + extent + col_at - 1)
            elif col_at == 0 and 1 <= row_at <= extent:
                entries.append(interior + 2 * extent + row_at - 1)
            elif col_at == padded_side - 1 and 1 <= row_at <= extent:
                entries.append(interior + 3 * extent + row_at - 1)
            else:
                corner = (0 if row_at == 0 else 2) + (0 if col_at == 0 else 1)
                entries.append(interior + 4 * extent + corner)
    return np.array(entries, np.int32)


def conv_layer(activity, kernel, local_beside, local_turns, gather_rims):
    length = 4 * P_SIZE - 4
    cycle_vals = jnp.take(activity, cycle_table(P_SIZE), axis=2)
    extended = gather_rims(cycle_vals)
    heading, anchor = border_tables(P_SIZE)
    near_tile = jnp.take(local_beside, heading, axis=1)
    near_turn = jnp.take(local_turns, heading, axis=1)
    source = near_tile * length + jnp.remainder(anchor[None, :] - near_turn * (P_SIZE - 1), length)
    flat_cycles = extended.reshape(extended.shape[0], -1)
    border = jnp.take(flat_cycles, source.reshape(-1), axis=1)
    border = border.reshape(activity.shape[0], activity.shape[1], 4 * P_SIZE + 4)
    joined = jnp.concatenate([activity, border], axis=2)
    padded = jnp.take(joined, layout_table(P_SIZE), axis=2)
    padded_side = P_SIZE + 2
    stretch = P_SIZE * padded_side - 2
    summed = None
    for tap_index in range(9):
        offset = padded_side + 1 + (tap_index // 3 - 1) * padded_side + (tap_index % 3 - 1)
        window = padded[:, :, offset : offset + stretch]
        partial_sum = jnp.einsum(
            "oc,ctq->otq", kernel[tap_index], window, preferred_element_type=jnp.float32
        )
        summed = partial_sum if summed is None else summed + partial_sum
    summed = jnp.pad(summed, ((0, 0), (0, 0), (0, 2)))
    summed = summed.reshape(summed.shape[0], summed.shape[1], P_SIZE, padded_side)[:, :, :, :P_SIZE]
    summed = summed.reshape(summed.shape[0], summed.shape[1], P_SIZE * P_SIZE)
    return jax.nn.gelu(summed, approximate=False).astype(jnp.bfloat16)


def on_device(
    analysis,
    send_rows,
    send_count,
    corner_slot,
    corner_weight,
    beside,
    quarter_turns,
    kernel_one,
    kernel_two,
    kernel_three,
):
    shards = lax.axis_size("tile")
    groups = lax.axis_size("chan")
    tiles_here = corner_slot.shape[1]
    near_count = send_rows.shape[1]
    capacity = send_rows.shape[2]
    channels_here = analysis.shape[0]
    pixels = corner_slot.shape[2]
    total_tiles = tiles_here * shards
    per_group = tiles_here // groups
    widths = [kernel_one.shape[2], kernel_two.shape[2], kernel_three.shape[2]]
    joined_kernels = jnp.concatenate([kernel_one, kernel_two, kernel_three], axis=2)
    joined_kernels = lax.all_gather(joined_kernels, "chan", axis=1, tiled=True)
    kernels = []
    low = 0
    for width in widths:
        kernels.append(joined_kernels[:, :, low : low + width])
        low += width
    slot_order = jnp.arange(capacity)
    rows_list = send_rows[0].reshape(-1)
    piece = jnp.take(analysis, rows_list, axis=1).reshape(channels_here, near_count, capacity)
    is_live = slot_order[None, :] < send_count[0][:, None]
    piece = jnp.where(is_live[None], piece, jnp.zeros((), piece.dtype))
    blocks = []
    for offset_index in range(near_count):
        block = piece[:, offset_index]
        if offset_index != REACH:
            block = from_behind(block, "tile", offset_index - REACH)
        blocks.append(block)
    arrived = jnp.stack(blocks, axis=1).reshape(channels_here, near_count * capacity)
    arrived = lax.all_gather(arrived, "chan", axis=0, tiled=True)
    group_index = lax.axis_index("chan")
    my_slots = lax.dynamic_slice_in_dim(corner_slot, group_index * per_group, per_group, 1)
    my_weights = lax.dynamic_slice_in_dim(corner_weight, group_index * per_group, per_group, 1)
    my_slots = my_slots.reshape(my_slots.shape[0], per_group * pixels)
    my_weights = my_weights.reshape(my_weights.shape[0], per_group * pixels)
    slot_ids = jnp.arange(near_count * capacity)
    summed = None
    for corner in range(my_slots.shape[0]):
        one_hot = (slot_ids[:, None] == my_slots[corner][None, :]).astype(arrived.dtype)
        picked = jnp.dot(arrived, one_hot, preferred_element_type=jnp.float32)
        term = picked * my_weights[corner][None, :]
        summed = term if summed is None else summed + term
    activity = summed.astype(jnp.bfloat16).reshape(arrived.shape[0], per_group, pixels)
    first_tile = lax.axis_index(("tile", "chan")) * per_group
    near_beside = lax.dynamic_slice_in_dim(beside, group_index * per_group, per_group, 0)
    near_turns = lax.dynamic_slice_in_dim(quarter_turns, group_index * per_group, per_group, 0)
    local_beside = jnp.remainder(near_beside - first_tile + REACH, total_tiles)

    def joined_rims(cycle_vals):
        return extended_2(cycle_vals, ((("tile", "chan"), 1),), REACH)

    for kernel in kernels:
        activity = conv_layer(activity, kernel, local_beside, near_turns, joined_rims)
    result = lax.all_to_all(activity, "chan", split_axis=0, concat_axis=1, tiled=True)
    return result


def solution(mesh):
    return jax.shard_map(
        on_device,
        mesh=mesh,
        in_specs=(
            P("chan", "tile"),
            P("tile", None, None),
            P("tile", None),
            P(None, "tile", None),
            P(None, "tile", None),
            P("tile", None),
            P("tile", None),
            P(None, "chan", None),
            P(None, "chan", None),
            P(None, "chan", None),
        ),
        out_specs=P("chan", "tile", None),
        check_vma=False,
    )
```

```python
import jax
import jax.numpy as jnp
import numpy as np
from jax import lax
from jax.sharding import PartitionSpec as P

P_SIZE = 16
REACH = 2


def from_behind(value, axis, steps):
    count = lax.axis_size(axis)
    pairs = [(source, (source + steps) % count) for source in range(count)]
    return lax.ppermute(value, axis, pairs)


def gather_by_exchange(value, axis, dim):
    count = lax.axis_size(axis)
    copies = jnp.concatenate([value] * count, axis=dim)
    return lax.all_to_all(copies, axis, split_axis=dim, concat_axis=dim, tiled=True)


def extended_2(x, sides, width):
    for axis, dim in sides:
        size, length = (lax.axis_size(axis), x.shape[dim])
        up = [(i, (i + 1) % size) for i in range(size)]
        down = [(j, i) for i, j in up]
        last = lax.slice_in_dim(x, length - width, length, axis=dim)
        initial = lax.slice_in_dim(x, 0, width, axis=dim)
        before = lax.ppermute(last, axis, up)
        after = lax.ppermute(initial, axis, down)
        x = jnp.concatenate([before, x, after], axis=dim)
    return x


def cycle_table(extent):
    length = 4 * extent - 4
    entries = []
    for cycle_pos in range(length):
        if cycle_pos < extent:
            row_at, col_at = (cycle_pos, 0)
        elif cycle_pos < 2 * extent - 1:
            row_at, col_at = (extent - 1, cycle_pos - extent + 1)
        elif cycle_pos < 3 * extent - 2:
            row_at, col_at = (3 * extent - 3 - cycle_pos, extent - 1)
        else:
            row_at, col_at = (0, 4 * extent - 4 - cycle_pos)
        entries.append(row_at * extent + col_at)
    return np.array(entries, np.int32)


def border_tables(extent):
    length = 4 * extent - 4
    heading = []
    anchor = []
    for col_at in range(extent):
        heading.append(0)
        anchor.append(extent - 1 + col_at)
    for col_at in range(extent):
        heading.append(1)
        anchor.append((length - col_at) % length)
    for row_at in range(extent):
        heading.append(2)
        anchor.append(3 * extent - 3 - row_at)
    for row_at in range(extent):
        heading.append(3)
        anchor.append(row_at)
    heading += [4, 5, 6, 7]
    anchor += [2 * extent - 2, extent - 1, 3 * extent - 3, 0]
    return (np.array(heading, np.int32), np.array(anchor, np.int32))


def layout_table(extent):
    padded_side = extent + 2
    interior = extent * extent
    entries = []
    for row_at in range(padded_side):
        for col_at in range(padded_side):
            if 1 <= row_at <= extent and 1 <= col_at <= extent:
                entries.append((row_at - 1) * extent + col_at - 1)
            elif row_at == 0 and 1 <= col_at <= extent:
                entries.append(interior + col_at - 1)
            elif row_at == padded_side - 1 and 1 <= col_at <= extent:
                entries.append(interior + extent + col_at - 1)
            elif col_at == 0 and 1 <= row_at <= extent:
                entries.append(interior + 2 * extent + row_at - 1)
            elif col_at == padded_side - 1 and 1 <= row_at <= extent:
                entries.append(interior + 3 * extent + row_at - 1)
            else:
                corner = (0 if row_at == 0 else 2) + (0 if col_at == 0 else 1)
                entries.append(interior + 4 * extent + corner)
    return np.array(entries, np.int32)


def conv_layer(activity, kernel, local_beside, local_turns, gather_rims):
    length = 4 * P_SIZE - 4
    cycle_vals = jnp.take(activity, cycle_table(P_SIZE), axis=2)
    extended = gather_rims(cycle_vals)
    heading, anchor = border_tables(P_SIZE)
    near_tile = jnp.take(local_beside, heading, axis=1)
    near_turn = jnp.take(local_turns, heading, axis=1)
    source = near_tile * length + jnp.remainder(anchor[None, :] - near_turn * (P_SIZE - 1), length)
    flat_cycles = extended.reshape(extended.shape[0], -1)
    border = jnp.take(flat_cycles, source.reshape(-1), axis=1)
    border = border.reshape(activity.shape[0], activity.shape[1], 4 * P_SIZE + 4)
    joined = jnp.concatenate([activity, border], axis=2)
    padded = jnp.take(joined, layout_table(P_SIZE), axis=2)
    padded_side = P_SIZE + 2
    stretch = P_SIZE * padded_side - 2
    summed = None
    for tap_index in range(9):
        offset = padded_side + 1 + (tap_index // 3 - 1) * padded_side + (tap_index % 3 - 1)
        window = padded[:, :, offset : offset + stretch]
        partial_sum = jnp.einsum(
            "oc,ctq->otq", kernel[tap_index], window, preferred_element_type=jnp.float32
        )
        summed = partial_sum if summed is None else summed + partial_sum
    summed = jnp.pad(summed, ((0, 0), (0, 0), (0, 2)))
    summed = summed.reshape(summed.shape[0], summed.shape[1], P_SIZE, padded_side)[:, :, :, :P_SIZE]
    summed = summed.reshape(summed.shape[0], summed.shape[1], P_SIZE * P_SIZE)
    return jax.nn.gelu(summed, approximate=False).astype(jnp.bfloat16)


def on_device(
    analysis,
    send_rows,
    send_count,
    corner_slot,
    corner_weight,
    beside,
    quarter_turns,
    kernel_one,
    kernel_two,
    kernel_three,
):
    shards = lax.axis_size("tile")
    groups = lax.axis_size("chan")
    tiles_here = corner_slot.shape[1]
    near_count = send_rows.shape[1]
    capacity = send_rows.shape[2]
    channels_here = analysis.shape[0]
    pixels = corner_slot.shape[2]
    total_tiles = tiles_here * shards
    per_group = tiles_here // groups
    widths = [kernel_one.shape[2], kernel_two.shape[2], kernel_three.shape[2]]
    joined_kernels = jnp.concatenate([kernel_one, kernel_two, kernel_three], axis=2)
    joined_kernels = gather_by_exchange(joined_kernels, "chan", 1)
    kernels = []
    low = 0
    for width in widths:
        kernels.append(joined_kernels[:, :, low : low + width])
        low += width
    slot_order = jnp.arange(capacity)
    rows_list = send_rows[0].reshape(-1)
    piece = jnp.take(analysis, rows_list, axis=1).reshape(channels_here, near_count, capacity)
    is_live = slot_order[None, :] < send_count[0][:, None]
    piece = jnp.where(is_live[None], piece, jnp.zeros((), piece.dtype))
    blocks = []
    for offset_index in range(near_count):
        block = piece[:, offset_index]
        if offset_index != REACH:
            block = from_behind(block, "tile", offset_index - REACH)
        blocks.append(block)
    arrived = jnp.stack(blocks, axis=1).reshape(channels_here, near_count * capacity)
    arrived = gather_by_exchange(arrived, "chan", 0)
    group_index = lax.axis_index("chan")
    my_slots = lax.dynamic_slice_in_dim(corner_slot, group_index * per_group, per_group, 1)
    my_weights = lax.dynamic_slice_in_dim(corner_weight, group_index * per_group, per_group, 1)
    my_slots = my_slots.reshape(my_slots.shape[0], per_group * pixels)
    my_weights = my_weights.reshape(my_weights.shape[0], per_group * pixels)
    slot_ids = jnp.arange(near_count * capacity)
    summed = None
    for corner in range(my_slots.shape[0]):
        one_hot = (slot_ids[:, None] == my_slots[corner][None, :]).astype(arrived.dtype)
        picked = jnp.dot(arrived, one_hot, preferred_element_type=jnp.float32)
        term = picked * my_weights[corner][None, :]
        summed = term if summed is None else summed + term
    activity = summed.astype(jnp.bfloat16).reshape(arrived.shape[0], per_group, pixels)
    first_tile = lax.axis_index(("tile", "chan")) * per_group
    near_beside = lax.dynamic_slice_in_dim(beside, group_index * per_group, per_group, 0)
    near_turns = lax.dynamic_slice_in_dim(quarter_turns, group_index * per_group, per_group, 0)
    local_beside = jnp.remainder(near_beside - first_tile + REACH, total_tiles)

    def joined_rims(cycle_vals):
        return extended_2(cycle_vals, ((("tile", "chan"), 1),), REACH)

    for kernel in kernels:
        activity = conv_layer(activity, kernel, local_beside, near_turns, joined_rims)
    result = lax.all_to_all(activity, "chan", split_axis=0, concat_axis=1, tiled=True)
    return result


def solution(mesh):
    return jax.shard_map(
        on_device,
        mesh=mesh,
        in_specs=(
            P("chan", "tile"),
            P("tile", None, None),
            P("tile", None),
            P(None, "tile", None),
            P(None, "tile", None),
            P("tile", None),
            P("tile", None),
            P(None, "chan", None),
            P(None, "chan", None),
            P(None, "chan", None),
        ),
        out_specs=P("chan", "tile", None),
        check_vma=False,
    )
```

```python
import jax
import jax.numpy as jnp
import numpy as np
from jax import lax
from jax.sharding import PartitionSpec as P

P_SIZE = 16
REACH = 2


def from_behind(value, axis, steps):
    count = lax.axis_size(axis)
    pairs = [(source, (source + steps) % count) for source in range(count)]
    return lax.ppermute(value, axis, pairs)


def gather_by_exchange(value, axis, dim):
    count = lax.axis_size(axis)
    copies = jnp.concatenate([value] * count, axis=dim)
    return lax.all_to_all(copies, axis, split_axis=dim, concat_axis=dim, tiled=True)


def extended_2(x, sides, width):
    for axis, dim in sides:
        size, length = (lax.axis_size(axis), x.shape[dim])
        up = [(i, (i + 1) % size) for i in range(size)]
        down = [(j, i) for i, j in up]
        last = lax.slice_in_dim(x, length - width, length, axis=dim)
        initial = lax.slice_in_dim(x, 0, width, axis=dim)
        before = lax.ppermute(last, axis, up)
        after = lax.ppermute(initial, axis, down)
        x = jnp.concatenate([before, x, after], axis=dim)
    return x


def cycle_table(extent):
    length = 4 * extent - 4
    entries = []
    for cycle_pos in range(length):
        if cycle_pos < extent:
            row_at, col_at = (cycle_pos, 0)
        elif cycle_pos < 2 * extent - 1:
            row_at, col_at = (extent - 1, cycle_pos - extent + 1)
        elif cycle_pos < 3 * extent - 2:
            row_at, col_at = (3 * extent - 3 - cycle_pos, extent - 1)
        else:
            row_at, col_at = (0, 4 * extent - 4 - cycle_pos)
        entries.append(row_at * extent + col_at)
    return np.array(entries, np.int32)


def border_tables(extent):
    length = 4 * extent - 4
    heading = []
    anchor = []
    for col_at in range(extent):
        heading.append(0)
        anchor.append(extent - 1 + col_at)
    for col_at in range(extent):
        heading.append(1)
        anchor.append((length - col_at) % length)
    for row_at in range(extent):
        heading.append(2)
        anchor.append(3 * extent - 3 - row_at)
    for row_at in range(extent):
        heading.append(3)
        anchor.append(row_at)
    heading += [4, 5, 6, 7]
    anchor += [2 * extent - 2, extent - 1, 3 * extent - 3, 0]
    return (np.array(heading, np.int32), np.array(anchor, np.int32))


def layout_table(extent):
    padded_side = extent + 2
    interior = extent * extent
    entries = []
    for row_at in range(padded_side):
        for col_at in range(padded_side):
            if 1 <= row_at <= extent and 1 <= col_at <= extent:
                entries.append((row_at - 1) * extent + col_at - 1)
            elif row_at == 0 and 1 <= col_at <= extent:
                entries.append(interior + col_at - 1)
            elif row_at == padded_side - 1 and 1 <= col_at <= extent:
                entries.append(interior + extent + col_at - 1)
            elif col_at == 0 and 1 <= row_at <= extent:
                entries.append(interior + 2 * extent + row_at - 1)
            elif col_at == padded_side - 1 and 1 <= row_at <= extent:
                entries.append(interior + 3 * extent + row_at - 1)
            else:
                corner = (0 if row_at == 0 else 2) + (0 if col_at == 0 else 1)
                entries.append(interior + 4 * extent + corner)
    return np.array(entries, np.int32)


def conv_layer(activity, kernel, local_beside, local_turns, gather_rims):
    length = 4 * P_SIZE - 4
    square = activity.reshape(activity.shape[0], activity.shape[1], P_SIZE, P_SIZE)
    cycle_vals = jnp.concatenate(
        [
            square[:, :, :, 0],
            square[:, :, P_SIZE - 1, 1:],
            square[:, :, P_SIZE - 2 :: -1, P_SIZE - 1],
            square[:, :, 0, P_SIZE - 2 : 0 : -1],
        ],
        axis=2,
    )
    extended = gather_rims(cycle_vals)
    heading, anchor = border_tables(P_SIZE)
    near_tile = jnp.take(local_beside, heading, axis=1)
    near_turn = jnp.take(local_turns, heading, axis=1)
    source = near_tile * length + jnp.remainder(anchor[None, :] - near_turn * (P_SIZE - 1), length)
    flat_cycles = extended.reshape(extended.shape[0], -1)
    border = jnp.take(flat_cycles, source.reshape(-1), axis=1)
    border = border.reshape(activity.shape[0], activity.shape[1], 4 * P_SIZE + 4)
    side = P_SIZE
    rims = [border[:, :, k * side : (k + 1) * side] for k in range(4)]
    corners = [border[:, :, 4 * side + k : 4 * side + k + 1] for k in range(4)]
    top_row = jnp.concatenate([corners[0], rims[0], corners[1]], axis=2)
    bottom_row = jnp.concatenate([corners[2], rims[1], corners[3]], axis=2)
    middle = jnp.concatenate([rims[2][..., None], square, rims[3][..., None]], axis=3)
    padded = jnp.concatenate([top_row[:, :, None], middle, bottom_row[:, :, None]], axis=2)
    padded_side = P_SIZE + 2
    padded = padded.reshape(activity.shape[0], activity.shape[1], padded_side * padded_side)
    stretch = P_SIZE * padded_side - 2
    summed = None
    for tap_index in range(9):
        offset = padded_side + 1 + (tap_index // 3 - 1) * padded_side + (tap_index % 3 - 1)
        window = padded[:, :, offset : offset + stretch]
        partial_sum = jnp.einsum(
            "oc,ctq->otq", kernel[tap_index], window, preferred_element_type=jnp.float32
        )
        summed = partial_sum if summed is None else summed + partial_sum
    summed = jnp.pad(summed, ((0, 0), (0, 0), (0, 2)))
    summed = summed.reshape(summed.shape[0], summed.shape[1], P_SIZE, padded_side)[:, :, :, :P_SIZE]
    summed = summed.reshape(summed.shape[0], summed.shape[1], P_SIZE * P_SIZE)
    return jax.nn.gelu(summed, approximate=False).astype(jnp.bfloat16)


def on_device(
    analysis,
    send_rows,
    send_count,
    corner_slot,
    corner_weight,
    beside,
    quarter_turns,
    kernel_one,
    kernel_two,
    kernel_three,
):
    shards = lax.axis_size("tile")
    groups = lax.axis_size("chan")
    tiles_here = corner_slot.shape[1]
    near_count = send_rows.shape[1]
    capacity = send_rows.shape[2]
    channels_here = analysis.shape[0]
    pixels = corner_slot.shape[2]
    total_tiles = tiles_here * shards
    per_group = tiles_here // groups
    widths = [kernel_one.shape[2], kernel_two.shape[2], kernel_three.shape[2]]
    joined_kernels = jnp.concatenate([kernel_one, kernel_two, kernel_three], axis=2)
    joined_kernels = gather_by_exchange(joined_kernels, "chan", 1)
    kernels = []
    low = 0
    for width in widths:
        kernels.append(joined_kernels[:, :, low : low + width])
        low += width
    slot_order = jnp.arange(capacity)
    rows_list = send_rows[0].reshape(-1)
    piece = jnp.take(analysis, rows_list, axis=1).reshape(channels_here, near_count, capacity)
    is_live = slot_order[None, :] < send_count[0][:, None]
    piece = jnp.where(is_live[None], piece, jnp.zeros((), piece.dtype))
    blocks = []
    for offset_index in range(near_count):
        block = piece[:, offset_index]
        if offset_index != REACH:
            block = from_behind(block, "tile", offset_index - REACH)
        blocks.append(block)
    arrived = jnp.stack(blocks, axis=1).reshape(channels_here, near_count * capacity)
    arrived = gather_by_exchange(arrived, "chan", 0)
    group_index = lax.axis_index("chan")
    my_slots = lax.dynamic_slice_in_dim(corner_slot, group_index * per_group, per_group, 1)
    my_weights = lax.dynamic_slice_in_dim(corner_weight, group_index * per_group, per_group, 1)
    my_slots = my_slots.reshape(my_slots.shape[0], per_group * pixels)
    my_weights = my_weights.reshape(my_weights.shape[0], per_group * pixels)
    slot_ids = jnp.arange(near_count * capacity)
    summed = None
    for corner in range(my_slots.shape[0]):
        one_hot = (slot_ids[:, None] == my_slots[corner][None, :]).astype(arrived.dtype)
        picked = jnp.dot(arrived, one_hot, preferred_element_type=jnp.float32)
        term = picked * my_weights[corner][None, :]
        summed = term if summed is None else summed + term
    activity = summed.astype(jnp.bfloat16).reshape(arrived.shape[0], per_group, pixels)
    first_tile = lax.axis_index(("tile", "chan")) * per_group
    near_beside = lax.dynamic_slice_in_dim(beside, group_index * per_group, per_group, 0)
    near_turns = lax.dynamic_slice_in_dim(quarter_turns, group_index * per_group, per_group, 0)
    local_beside = jnp.remainder(near_beside - first_tile + REACH, total_tiles)

    def joined_rims(cycle_vals):
        return extended_2(cycle_vals, ((("tile", "chan"), 1),), REACH)

    for kernel in kernels:
        activity = conv_layer(activity, kernel, local_beside, near_turns, joined_rims)
    result = lax.all_to_all(activity, "chan", split_axis=0, concat_axis=1, tiled=True)
    return result


def solution(mesh):
    return jax.shard_map(
        on_device,
        mesh=mesh,
        in_specs=(
            P("chan", "tile"),
            P("tile", None, None),
            P("tile", None),
            P(None, "tile", None),
            P(None, "tile", None),
            P("tile", None),
            P("tile", None),
            P(None, "chan", None),
            P(None, "chan", None),
            P(None, "chan", None),
        ),
        out_specs=P("chan", "tile", None),
        check_vma=False,
    )
```

```python
import jax
import jax.numpy as jnp
import numpy as np
from jax import lax
from jax.sharding import PartitionSpec as P

P_SIZE = 16
REACH = 2


def from_behind(value, axis, steps):
    count = lax.axis_size(axis)
    pairs = [(source, (source + steps) % count) for source in range(count)]
    return lax.ppermute(value, axis, pairs)


def gather_by_exchange(value, axis, dim):
    count = lax.axis_size(axis)
    copies = jnp.concatenate([value] * count, axis=dim)
    return lax.all_to_all(copies, axis, split_axis=dim, concat_axis=dim, tiled=True)


def extended_2(x, sides, width):
    for axis, dim in sides:
        size, length = (lax.axis_size(axis), x.shape[dim])
        up = [(i, (i + 1) % size) for i in range(size)]
        down = [(j, i) for i, j in up]
        last = lax.slice_in_dim(x, length - width, length, axis=dim)
        initial = lax.slice_in_dim(x, 0, width, axis=dim)
        before = lax.ppermute(last, axis, up)
        after = lax.ppermute(initial, axis, down)
        x = jnp.concatenate([before, x, after], axis=dim)
    return x


def cycle_table(extent):
    length = 4 * extent - 4
    entries = []
    for cycle_pos in range(length):
        if cycle_pos < extent:
            row_at, col_at = (cycle_pos, 0)
        elif cycle_pos < 2 * extent - 1:
            row_at, col_at = (extent - 1, cycle_pos - extent + 1)
        elif cycle_pos < 3 * extent - 2:
            row_at, col_at = (3 * extent - 3 - cycle_pos, extent - 1)
        else:
            row_at, col_at = (0, 4 * extent - 4 - cycle_pos)
        entries.append(row_at * extent + col_at)
    return np.array(entries, np.int32)


def border_tables(extent):
    length = 4 * extent - 4
    heading = []
    anchor = []
    for col_at in range(extent):
        heading.append(0)
        anchor.append(extent - 1 + col_at)
    for col_at in range(extent):
        heading.append(1)
        anchor.append((length - col_at) % length)
    for row_at in range(extent):
        heading.append(2)
        anchor.append(3 * extent - 3 - row_at)
    for row_at in range(extent):
        heading.append(3)
        anchor.append(row_at)
    heading += [4, 5, 6, 7]
    anchor += [2 * extent - 2, extent - 1, 3 * extent - 3, 0]
    return (np.array(heading, np.int32), np.array(anchor, np.int32))


def layout_table(extent):
    padded_side = extent + 2
    interior = extent * extent
    entries = []
    for row_at in range(padded_side):
        for col_at in range(padded_side):
            if 1 <= row_at <= extent and 1 <= col_at <= extent:
                entries.append((row_at - 1) * extent + col_at - 1)
            elif row_at == 0 and 1 <= col_at <= extent:
                entries.append(interior + col_at - 1)
            elif row_at == padded_side - 1 and 1 <= col_at <= extent:
                entries.append(interior + extent + col_at - 1)
            elif col_at == 0 and 1 <= row_at <= extent:
                entries.append(interior + 2 * extent + row_at - 1)
            elif col_at == padded_side - 1 and 1 <= row_at <= extent:
                entries.append(interior + 3 * extent + row_at - 1)
            else:
                corner = (0 if row_at == 0 else 2) + (0 if col_at == 0 else 1)
                entries.append(interior + 4 * extent + corner)
    return np.array(entries, np.int32)


def conv_layer(activity, kernel, local_beside, local_turns, gather_rims):
    length = 4 * P_SIZE - 4
    cycle_vals = jnp.take(activity, cycle_table(P_SIZE), axis=2)
    extended = gather_rims(cycle_vals)
    heading, anchor = border_tables(P_SIZE)
    near_tile = jnp.take(local_beside, heading, axis=1)
    near_turn = jnp.take(local_turns, heading, axis=1)
    source = near_tile * length + jnp.remainder(anchor[None, :] - near_turn * (P_SIZE - 1), length)
    flat_cycles = extended.reshape(extended.shape[0], -1)
    border = jnp.take(flat_cycles, source.reshape(-1), axis=1)
    border = border.reshape(activity.shape[0], activity.shape[1], 4 * P_SIZE + 4)
    joined = jnp.concatenate([activity, border], axis=2)
    padded = jnp.take(joined, layout_table(P_SIZE), axis=2)
    padded_side = P_SIZE + 2
    stretch = P_SIZE * padded_side - 2
    summed = None
    for tap_index in range(9):
        offset = padded_side + 1 + (tap_index // 3 - 1) * padded_side + (tap_index % 3 - 1)
        window = padded[:, :, offset : offset + stretch]
        partial_sum = jnp.einsum(
            "oc,ctq->otq", kernel[tap_index], window, preferred_element_type=jnp.float32
        )
        summed = partial_sum if summed is None else summed + partial_sum
    summed = jnp.pad(summed, ((0, 0), (0, 0), (0, 2)))
    summed = summed.reshape(summed.shape[0], summed.shape[1], P_SIZE, padded_side)[:, :, :, :P_SIZE]
    summed = summed.reshape(summed.shape[0], summed.shape[1], P_SIZE * P_SIZE)
    return jax.nn.gelu(summed, approximate=False).astype(jnp.bfloat16)


def on_device(
    analysis,
    send_rows,
    send_count,
    corner_slot,
    corner_weight,
    beside,
    quarter_turns,
    kernel_one,
    kernel_two,
    kernel_three,
):
    shards = lax.axis_size("tile")
    groups = lax.axis_size("chan")
    tiles_here = corner_slot.shape[1]
    near_count = send_rows.shape[1]
    capacity = send_rows.shape[2]
    channels_here = analysis.shape[0]
    pixels = corner_slot.shape[2]
    total_tiles = tiles_here * shards
    per_group = tiles_here // groups
    widths = [kernel_one.shape[2], kernel_two.shape[2], kernel_three.shape[2]]
    joined_kernels = jnp.concatenate([kernel_one, kernel_two, kernel_three], axis=2)
    joined_kernels = gather_by_exchange(joined_kernels, "chan", 1)
    kernels = []
    low = 0
    for width in widths:
        kernels.append(joined_kernels[:, :, low : low + width])
        low += width
    slot_order = jnp.arange(capacity)
    blocks = []
    for offset_index in range(near_count):
        block = jnp.take(analysis, send_rows[0, offset_index], axis=1)
        is_live = slot_order < send_count[0, offset_index]
        block = jnp.where(is_live[None, :], block, jnp.zeros((), block.dtype))
        if offset_index != REACH:
            block = from_behind(block, "tile", offset_index - REACH)
        blocks.append(block)
    arrived = jnp.stack(blocks, axis=1).reshape(channels_here, near_count * capacity)
    arrived = gather_by_exchange(arrived, "chan", 0)
    group_index = lax.axis_index("chan")
    my_slots = lax.dynamic_slice_in_dim(corner_slot, group_index * per_group, per_group, 1)
    my_weights = lax.dynamic_slice_in_dim(corner_weight, group_index * per_group, per_group, 1)
    my_slots = my_slots.reshape(my_slots.shape[0], per_group * pixels)
    my_weights = my_weights.reshape(my_weights.shape[0], per_group * pixels)
    slot_ids = jnp.arange(near_count * capacity)
    summed = None
    for corner in range(my_slots.shape[0]):
        one_hot = (slot_ids[:, None] == my_slots[corner][None, :]).astype(arrived.dtype)
        picked = jnp.dot(arrived, one_hot, preferred_element_type=jnp.float32)
        term = picked * my_weights[corner][None, :]
        summed = term if summed is None else summed + term
    activity = summed.astype(jnp.bfloat16).reshape(arrived.shape[0], per_group, pixels)
    first_tile = lax.axis_index(("tile", "chan")) * per_group
    near_beside = lax.dynamic_slice_in_dim(beside, group_index * per_group, per_group, 0)
    near_turns = lax.dynamic_slice_in_dim(quarter_turns, group_index * per_group, per_group, 0)
    local_beside = jnp.remainder(near_beside - first_tile + REACH, total_tiles)

    def joined_rims(cycle_vals):
        return extended_2(cycle_vals, ((("tile", "chan"), 1),), REACH)

    for kernel in kernels:
        activity = conv_layer(activity, kernel, local_beside, near_turns, joined_rims)
    result = lax.all_to_all(activity, "chan", split_axis=0, concat_axis=1, tiled=True)
    return result


def solution(mesh):
    step = jax.shard_map(
        on_device,
        mesh=mesh,
        in_specs=(
            P("chan", "tile"),
            P("tile", None, None),
            P("tile", None),
            P(None, "tile", None),
            P(None, "tile", None),
            P("tile", None),
            P("tile", None),
            P(None, "chan", None),
            P(None, "chan", None),
            P(None, "chan", None),
        ),
        out_specs=P("chan", "tile", None),
        check_vma=False,
    )
    return step
```

```python
import jax
import jax.numpy as jnp
import numpy as np
from jax import lax
from jax.sharding import PartitionSpec as P

P_SIZE = 16
REACH = 2


def from_behind(value, axis, steps):
    count = lax.axis_size(axis)
    pairs = [(source, (source + steps) % count) for source in range(count)]
    return lax.ppermute(value, axis, pairs)


def gather_by_exchange(value, axis, dim):
    count = lax.axis_size(axis)
    shape = value.shape
    copies = jnp.broadcast_to(
        jnp.expand_dims(value, dim), shape[:dim] + (count,) + shape[dim:]
    )
    copies = copies.reshape(shape[:dim] + (count * shape[dim],) + shape[dim + 1 :])
    return lax.all_to_all(copies, axis, split_axis=dim, concat_axis=dim, tiled=True)


def extended_2(x, sides, width):
    for axis, dim in sides:
        size, length = (lax.axis_size(axis), x.shape[dim])
        up = [(i, (i + 1) % size) for i in range(size)]
        down = [(j, i) for i, j in up]
        last = lax.slice_in_dim(x, length - width, length, axis=dim)
        initial = lax.slice_in_dim(x, 0, width, axis=dim)
        before = lax.ppermute(last, axis, up)
        after = lax.ppermute(initial, axis, down)
        x = jnp.concatenate([before, x, after], axis=dim)
    return x


def cycle_table(extent):
    length = 4 * extent - 4
    entries = []
    for cycle_pos in range(length):
        if cycle_pos < extent:
            row_at, col_at = (cycle_pos, 0)
        elif cycle_pos < 2 * extent - 1:
            row_at, col_at = (extent - 1, cycle_pos - extent + 1)
        elif cycle_pos < 3 * extent - 2:
            row_at, col_at = (3 * extent - 3 - cycle_pos, extent - 1)
        else:
            row_at, col_at = (0, 4 * extent - 4 - cycle_pos)
        entries.append(row_at * extent + col_at)
    return np.array(entries, np.int32)


def border_tables(extent):
    length = 4 * extent - 4
    heading = []
    anchor = []
    for col_at in range(extent):
        heading.append(0)
        anchor.append(extent - 1 + col_at)
    for col_at in range(extent):
        heading.append(1)
        anchor.append((length - col_at) % length)
    for row_at in range(extent):
        heading.append(2)
        anchor.append(3 * extent - 3 - row_at)
    for row_at in range(extent):
        heading.append(3)
        anchor.append(row_at)
    heading += [4, 5, 6, 7]
    anchor += [2 * extent - 2, extent - 1, 3 * extent - 3, 0]
    return (np.array(heading, np.int32), np.array(anchor, np.int32))


def layout_table(extent):
    padded_side = extent + 2
    interior = extent * extent
    entries = []
    for row_at in range(padded_side):
        for col_at in range(padded_side):
            if 1 <= row_at <= extent and 1 <= col_at <= extent:
                entries.append((row_at - 1) * extent + col_at - 1)
            elif row_at == 0 and 1 <= col_at <= extent:
                entries.append(interior + col_at - 1)
            elif row_at == padded_side - 1 and 1 <= col_at <= extent:
                entries.append(interior + extent + col_at - 1)
            elif col_at == 0 and 1 <= row_at <= extent:
                entries.append(interior + 2 * extent + row_at - 1)
            elif col_at == padded_side - 1 and 1 <= row_at <= extent:
                entries.append(interior + 3 * extent + row_at - 1)
            else:
                corner = (0 if row_at == 0 else 2) + (0 if col_at == 0 else 1)
                entries.append(interior + 4 * extent + corner)
    return np.array(entries, np.int32)


def conv_layer(activity, kernel, local_beside, local_turns, gather_rims):
    length = 4 * P_SIZE - 4
    cycle_vals = jnp.take(activity, cycle_table(P_SIZE), axis=2)
    extended = gather_rims(cycle_vals)
    heading, anchor = border_tables(P_SIZE)
    near_tile = jnp.take(local_beside, heading, axis=1)
    near_turn = jnp.take(local_turns, heading, axis=1)
    source = near_tile * length + jnp.remainder(anchor[None, :] - near_turn * (P_SIZE - 1), length)
    flat_cycles = extended.reshape(extended.shape[0], -1)
    border = jnp.take(flat_cycles, source.reshape(-1), axis=1)
    border = border.reshape(activity.shape[0], activity.shape[1], 4 * P_SIZE + 4)
    joined = jnp.concatenate([activity, border], axis=2)
    padded = jnp.take(joined, layout_table(P_SIZE), axis=2)
    padded_side = P_SIZE + 2
    stretch = P_SIZE * padded_side - 2
    summed = None
    for tap_index in range(9):
        offset = padded_side + 1 + (tap_index // 3 - 1) * padded_side + (tap_index % 3 - 1)
        window = padded[:, :, offset : offset + stretch]
        partial_sum = jnp.einsum(
            "oc,ctq->otq", kernel[tap_index], window, preferred_element_type=jnp.float32
        )
        summed = partial_sum if summed is None else summed + partial_sum
    summed = jnp.pad(summed, ((0, 0), (0, 0), (0, 2)))
    summed = summed.reshape(summed.shape[0], summed.shape[1], P_SIZE, padded_side)[:, :, :, :P_SIZE]
    summed = summed.reshape(summed.shape[0], summed.shape[1], P_SIZE * P_SIZE)
    return jax.nn.gelu(summed, approximate=False).astype(jnp.bfloat16)


def on_device(
    analysis,
    send_rows,
    send_count,
    corner_slot,
    corner_weight,
    beside,
    quarter_turns,
    kernel_one,
    kernel_two,
    kernel_three,
):
    shards = lax.axis_size("tile")
    groups = lax.axis_size("chan")
    tiles_here = corner_slot.shape[1]
    near_count = send_rows.shape[1]
    capacity = send_rows.shape[2]
    channels_here = analysis.shape[0]
    pixels = corner_slot.shape[2]
    total_tiles = tiles_here * shards
    per_group = tiles_here // groups
    widths = [kernel_one.shape[2], kernel_two.shape[2], kernel_three.shape[2]]
    joined_kernels = jnp.concatenate([kernel_one, kernel_two, kernel_three], axis=2)
    joined_kernels = gather_by_exchange(joined_kernels, "chan", 1)
    kernels = []
    low = 0
    for width in widths:
        kernels.append(joined_kernels[:, :, low : low + width])
        low += width
    slot_order = jnp.arange(capacity)
    blocks = []
    for offset_index in range(near_count):
        block = jnp.take(analysis, send_rows[0, offset_index], axis=1)
        is_live = slot_order < send_count[0, offset_index]
        block = jnp.where(is_live[None, :], block, jnp.zeros((), block.dtype))
        if offset_index != REACH:
            block = from_behind(block, "tile", offset_index - REACH)
        blocks.append(block)
    arrived = jnp.concatenate(blocks, axis=1)
    arrived = gather_by_exchange(arrived, "chan", 0)
    group_index = lax.axis_index("chan")
    my_slots = lax.dynamic_slice_in_dim(corner_slot, group_index * per_group, per_group, 1)
    my_weights = lax.dynamic_slice_in_dim(corner_weight, group_index * per_group, per_group, 1)
    my_slots = my_slots.reshape(my_slots.shape[0], per_group * pixels)
    my_weights = my_weights.reshape(my_weights.shape[0], per_group * pixels)
    slot_ids = jnp.arange(near_count * capacity)
    summed = None
    for corner in range(my_slots.shape[0]):
        one_hot = (slot_ids[:, None] == my_slots[corner][None, :]).astype(arrived.dtype)
        picked = jnp.dot(arrived, one_hot, preferred_element_type=jnp.float32)
        term = picked * my_weights[corner][None, :]
        summed = term if summed is None else summed + term
    activity = summed.astype(jnp.bfloat16).reshape(arrived.shape[0], per_group, pixels)
    first_tile = lax.axis_index(("tile", "chan")) * per_group
    near_beside = lax.dynamic_slice_in_dim(beside, group_index * per_group, per_group, 0)
    near_turns = lax.dynamic_slice_in_dim(quarter_turns, group_index * per_group, per_group, 0)
    local_beside = jnp.remainder(near_beside - first_tile + REACH, total_tiles)

    def joined_rims(cycle_vals):
        return extended_2(cycle_vals, ((("tile", "chan"), 1),), REACH)

    for kernel in kernels:
        activity = conv_layer(activity, kernel, local_beside, near_turns, joined_rims)
    result = lax.all_to_all(activity, "chan", split_axis=0, concat_axis=1, tiled=True)
    return result


def solution(mesh):
    step = jax.shard_map(
        on_device,
        mesh=mesh,
        in_specs=(
            P("chan", "tile"),
            P("tile", None, None),
            P("tile", None),
            P(None, "tile", None),
            P(None, "tile", None),
            P("tile", None),
            P("tile", None),
            P(None, "chan", None),
            P(None, "chan", None),
            P(None, "chan", None),
        ),
        out_specs=P("chan", "tile", None),
        check_vma=False,
    )
    return step
```

```python
import jax
import jax.numpy as jnp
import numpy as np
from jax import lax
from jax.sharding import PartitionSpec as P

P_SIZE = 16
REACH = 2


def from_behind(value, axis, steps):
    count = lax.axis_size(axis)
    pairs = [(source, (source + steps) % count) for source in range(count)]
    return lax.ppermute(value, axis, pairs)


def gather_by_exchange(value, axis, dim):
    count = lax.axis_size(axis)
    shape = value.shape
    copies = jnp.broadcast_to(
        jnp.expand_dims(value, dim), shape[:dim] + (count,) + shape[dim:]
    )
    copies = copies.reshape(shape[:dim] + (count * shape[dim],) + shape[dim + 1 :])
    return lax.all_to_all(copies, axis, split_axis=dim, concat_axis=dim, tiled=True)


def extended_2(x, sides, width):
    for axis, dim in sides:
        size, length = (lax.axis_size(axis), x.shape[dim])
        up = [(i, (i + 1) % size) for i in range(size)]
        down = [(j, i) for i, j in up]
        last = lax.slice_in_dim(x, length - width, length, axis=dim)
        initial = lax.slice_in_dim(x, 0, width, axis=dim)
        before = lax.ppermute(last, axis, up)
        after = lax.ppermute(initial, axis, down)
        x = jnp.concatenate([before, x, after], axis=dim)
    return x


def cycle_table(extent):
    length = 4 * extent - 4
    entries = []
    for cycle_pos in range(length):
        if cycle_pos < extent:
            row_at, col_at = (cycle_pos, 0)
        elif cycle_pos < 2 * extent - 1:
            row_at, col_at = (extent - 1, cycle_pos - extent + 1)
        elif cycle_pos < 3 * extent - 2:
            row_at, col_at = (3 * extent - 3 - cycle_pos, extent - 1)
        else:
            row_at, col_at = (0, 4 * extent - 4 - cycle_pos)
        entries.append(row_at * extent + col_at)
    return np.array(entries, np.int32)


def border_tables(extent):
    length = 4 * extent - 4
    heading = []
    anchor = []
    for col_at in range(extent):
        heading.append(0)
        anchor.append(extent - 1 + col_at)
    for col_at in range(extent):
        heading.append(1)
        anchor.append((length - col_at) % length)
    for row_at in range(extent):
        heading.append(2)
        anchor.append(3 * extent - 3 - row_at)
    for row_at in range(extent):
        heading.append(3)
        anchor.append(row_at)
    heading += [4, 5, 6, 7]
    anchor += [2 * extent - 2, extent - 1, 3 * extent - 3, 0]
    return (np.array(heading, np.int32), np.array(anchor, np.int32))


def layout_table(extent):
    padded_side = extent + 2
    interior = extent * extent
    entries = []
    for row_at in range(padded_side):
        for col_at in range(padded_side):
            if 1 <= row_at <= extent and 1 <= col_at <= extent:
                entries.append((row_at - 1) * extent + col_at - 1)
            elif row_at == 0 and 1 <= col_at <= extent:
                entries.append(interior + col_at - 1)
            elif row_at == padded_side - 1 and 1 <= col_at <= extent:
                entries.append(interior + extent + col_at - 1)
            elif col_at == 0 and 1 <= row_at <= extent:
                entries.append(interior + 2 * extent + row_at - 1)
            elif col_at == padded_side - 1 and 1 <= row_at <= extent:
                entries.append(interior + 3 * extent + row_at - 1)
            else:
                corner = (0 if row_at == 0 else 2) + (0 if col_at == 0 else 1)
                entries.append(interior + 4 * extent + corner)
    return np.array(entries, np.int32)


def conv_layer(activity, kernel, local_beside, local_turns, gather_rims):
    length = 4 * P_SIZE - 4
    cycle_vals = jnp.take(activity, cycle_table(P_SIZE), axis=2)
    extended = gather_rims(cycle_vals)
    heading, anchor = border_tables(P_SIZE)
    near_tile = jnp.take(local_beside, heading, axis=1)
    near_turn = jnp.take(local_turns, heading, axis=1)
    source = near_tile * length + jnp.remainder(anchor[None, :] - near_turn * (P_SIZE - 1), length)
    flat_cycles = extended.reshape(extended.shape[0], -1)
    border = jnp.take(flat_cycles, source.reshape(-1), axis=1)
    border = border.reshape(activity.shape[0], activity.shape[1], 4 * P_SIZE + 4)
    joined = jnp.concatenate([activity, border], axis=2)
    padded = jnp.take(joined, layout_table(P_SIZE), axis=2)
    padded_side = P_SIZE + 2
    stretch = P_SIZE * padded_side - 2
    summed = None
    for tap_index in range(9):
        offset = padded_side + 1 + (tap_index // 3 - 1) * padded_side + (tap_index % 3 - 1)
        window = padded[:, :, offset : offset + stretch]
        partial_sum = jnp.einsum(
            "oc,ctq->otq", kernel[tap_index], window, preferred_element_type=jnp.float32
        )
        summed = partial_sum if summed is None else summed + partial_sum
    summed = jnp.pad(summed, ((0, 0), (0, 0), (0, 2)))
    summed = summed.reshape(summed.shape[0], summed.shape[1], P_SIZE, padded_side)[:, :, :, :P_SIZE]
    summed = summed.reshape(summed.shape[0], summed.shape[1], P_SIZE * P_SIZE)
    return jax.nn.gelu(summed, approximate=False).astype(jnp.bfloat16)


def on_device(
    analysis,
    send_rows,
    send_count,
    corner_slot,
    corner_weight,
    beside,
    quarter_turns,
    kernel_one,
    kernel_two,
    kernel_three,
):
    shards = lax.axis_size("tile")
    groups = lax.axis_size("chan")
    tiles_here = corner_slot.shape[1]
    near_count = send_rows.shape[1]
    capacity = send_rows.shape[2]
    channels_here = analysis.shape[0]
    pixels = corner_slot.shape[2]
    total_tiles = tiles_here * shards
    per_group = tiles_here // groups
    widths = [kernel_one.shape[2], kernel_two.shape[2], kernel_three.shape[2]]
    joined_kernels = jnp.concatenate([kernel_one, kernel_two, kernel_three], axis=2)
    slot_order = jnp.arange(capacity)
    picked = []
    for offset_index in range(near_count):
        block = jnp.take(analysis, send_rows[0, offset_index], axis=1)
        is_live = slot_order < send_count[0, offset_index]
        picked.append(jnp.where(is_live[None, :], block, jnp.zeros((), block.dtype)))
    pieces = jnp.concatenate(picked, axis=1)
    piece_size = pieces.size
    payload = jnp.concatenate([pieces.reshape(-1), joined_kernels.reshape(-1)])
    received = gather_by_exchange(payload[None], "chan", 0)
    pieces = received[:, :piece_size].reshape(groups * channels_here, near_count * capacity)
    joined_kernels = received[:, piece_size:].reshape((groups,) + joined_kernels.shape)
    joined_kernels = jnp.transpose(joined_kernels, (1, 0, 2, 3))
    joined_kernels = joined_kernels.reshape(
        joined_kernels.shape[0], groups * joined_kernels.shape[2], joined_kernels.shape[3]
    )
    kernels = []
    low = 0
    for width in widths:
        kernels.append(joined_kernels[:, :, low : low + width])
        low += width
    blocks = []
    for offset_index in range(near_count):
        block = pieces[:, offset_index * capacity : (offset_index + 1) * capacity]
        if offset_index != REACH:
            block = from_behind(block, "tile", offset_index - REACH)
        blocks.append(block)
    arrived = jnp.concatenate(blocks, axis=1)
    group_index = lax.axis_index("chan")
    my_slots = lax.dynamic_slice_in_dim(corner_slot, group_index * per_group, per_group, 1)
    my_weights = lax.dynamic_slice_in_dim(corner_weight, group_index * per_group, per_group, 1)
    my_slots = my_slots.reshape(my_slots.shape[0], per_group * pixels)
    my_weights = my_weights.reshape(my_weights.shape[0], per_group * pixels)
    slot_ids = jnp.arange(near_count * capacity)
    summed = None
    for corner in range(my_slots.shape[0]):
        one_hot = (slot_ids[:, None] == my_slots[corner][None, :]).astype(arrived.dtype)
        picked = jnp.dot(arrived, one_hot, preferred_element_type=jnp.float32)
        term = picked * my_weights[corner][None, :]
        summed = term if summed is None else summed + term
    activity = summed.astype(jnp.bfloat16).reshape(arrived.shape[0], per_group, pixels)
    first_tile = lax.axis_index(("tile", "chan")) * per_group
    near_beside = lax.dynamic_slice_in_dim(beside, group_index * per_group, per_group, 0)
    near_turns = lax.dynamic_slice_in_dim(quarter_turns, group_index * per_group, per_group, 0)
    local_beside = jnp.remainder(near_beside - first_tile + REACH, total_tiles)

    def joined_rims(cycle_vals):
        return extended_2(cycle_vals, ((("tile", "chan"), 1),), REACH)

    for kernel in kernels:
        activity = conv_layer(activity, kernel, local_beside, near_turns, joined_rims)
    result = lax.all_to_all(activity, "chan", split_axis=0, concat_axis=1, tiled=True)
    return result


def solution(mesh):
    step = jax.shard_map(
        on_device,
        mesh=mesh,
        in_specs=(
            P("chan", "tile"),
            P("tile", None, None),
            P("tile", None),
            P(None, "tile", None),
            P(None, "tile", None),
            P("tile", None),
            P("tile", None),
            P(None, "chan", None),
            P(None, "chan", None),
            P(None, "chan", None),
        ),
        out_specs=P("chan", "tile", None),
        check_vma=False,
    )
    return step
```

```python
import jax
import jax.numpy as jnp
import numpy as np
from jax import lax
from jax.sharding import PartitionSpec as P

P_SIZE = 16
REACH = 2


def from_behind(value, axis, steps):
    count = lax.axis_size(axis)
    pairs = [(source, (source + steps) % count) for source in range(count)]
    return lax.ppermute(value, axis, pairs)


def gather_by_exchange(value, axis, dim):
    count = lax.axis_size(axis)
    shape = value.shape
    copies = jnp.broadcast_to(
        jnp.expand_dims(value, dim), shape[:dim] + (count,) + shape[dim:]
    )
    copies = copies.reshape(shape[:dim] + (count * shape[dim],) + shape[dim + 1 :])
    return lax.all_to_all(copies, axis, split_axis=dim, concat_axis=dim, tiled=True)


def extended_2(x, sides, width):
    for axis, dim in sides:
        size, length = (lax.axis_size(axis), x.shape[dim])
        up = [(i, (i + 1) % size) for i in range(size)]
        down = [(j, i) for i, j in up]
        last = lax.slice_in_dim(x, length - width, length, axis=dim)
        initial = lax.slice_in_dim(x, 0, width, axis=dim)
        before = lax.ppermute(last, axis, up)
        after = lax.ppermute(initial, axis, down)
        x = jnp.concatenate([before, x, after], axis=dim)
    return x


def cycle_table(extent):
    length = 4 * extent - 4
    entries = []
    for cycle_pos in range(length):
        if cycle_pos < extent:
            row_at, col_at = (cycle_pos, 0)
        elif cycle_pos < 2 * extent - 1:
            row_at, col_at = (extent - 1, cycle_pos - extent + 1)
        elif cycle_pos < 3 * extent - 2:
            row_at, col_at = (3 * extent - 3 - cycle_pos, extent - 1)
        else:
            row_at, col_at = (0, 4 * extent - 4 - cycle_pos)
        entries.append(row_at * extent + col_at)
    return np.array(entries, np.int32)


def border_tables(extent):
    length = 4 * extent - 4
    heading = []
    anchor = []
    for col_at in range(extent):
        heading.append(0)
        anchor.append(extent - 1 + col_at)
    for col_at in range(extent):
        heading.append(1)
        anchor.append((length - col_at) % length)
    for row_at in range(extent):
        heading.append(2)
        anchor.append(3 * extent - 3 - row_at)
    for row_at in range(extent):
        heading.append(3)
        anchor.append(row_at)
    heading += [4, 5, 6, 7]
    anchor += [2 * extent - 2, extent - 1, 3 * extent - 3, 0]
    return (np.array(heading, np.int32), np.array(anchor, np.int32))


def layout_table(extent):
    padded_side = extent + 2
    interior = extent * extent
    entries = []
    for row_at in range(padded_side):
        for col_at in range(padded_side):
            if 1 <= row_at <= extent and 1 <= col_at <= extent:
                entries.append((row_at - 1) * extent + col_at - 1)
            elif row_at == 0 and 1 <= col_at <= extent:
                entries.append(interior + col_at - 1)
            elif row_at == padded_side - 1 and 1 <= col_at <= extent:
                entries.append(interior + extent + col_at - 1)
            elif col_at == 0 and 1 <= row_at <= extent:
                entries.append(interior + 2 * extent + row_at - 1)
            elif col_at == padded_side - 1 and 1 <= row_at <= extent:
                entries.append(interior + 3 * extent + row_at - 1)
            else:
                corner = (0 if row_at == 0 else 2) + (0 if col_at == 0 else 1)
                entries.append(interior + 4 * extent + corner)
    return np.array(entries, np.int32)


def padded_index(tiles, local_beside, local_turns):
    length = 4 * P_SIZE - 4
    interior = P_SIZE * P_SIZE
    heading, anchor = border_tables(P_SIZE)
    near_tile = jnp.take(local_beside, heading, axis=1)
    near_turn = jnp.take(local_turns, heading, axis=1)
    source = near_tile * length + jnp.remainder(anchor[None, :] - near_turn * (P_SIZE - 1), length)
    layout = layout_table(P_SIZE)
    tile_ids = jnp.arange(tiles)[:, None]
    from_interior = tile_ids * interior + jnp.minimum(layout, interior - 1)[None, :]
    border_at = np.maximum(layout - interior, 0)
    from_border = tiles * interior + jnp.take(source, border_at, axis=1)
    return jnp.where((layout < interior)[None, :], from_interior, from_border)


def conv_layer(activity, kernel, where_from, gather_rims):
    cycle_vals = jnp.take(activity, cycle_table(P_SIZE), axis=2)
    extended = gather_rims(cycle_vals)
    channels, tiles = activity.shape[0], activity.shape[1]
    joined = jnp.concatenate(
        [activity.reshape(channels, -1), extended.reshape(channels, -1)], axis=1
    )
    padded = jnp.take(joined, where_from.reshape(-1), axis=1).reshape(channels, tiles, -1)
    padded_side = P_SIZE + 2
    stretch = P_SIZE * padded_side - 2
    summed = None
    for tap_index in range(9):
        offset = padded_side + 1 + (tap_index // 3 - 1) * padded_side + (tap_index % 3 - 1)
        window = padded[:, :, offset : offset + stretch]
        partial_sum = jnp.einsum(
            "oc,ctq->otq", kernel[tap_index], window, preferred_element_type=jnp.float32
        )
        summed = partial_sum if summed is None else summed + partial_sum
    summed = jnp.pad(summed, ((0, 0), (0, 0), (0, 2)))
    summed = summed.reshape(summed.shape[0], summed.shape[1], P_SIZE, padded_side)[:, :, :, :P_SIZE]
    summed = summed.reshape(summed.shape[0], summed.shape[1], P_SIZE * P_SIZE)
    return jax.nn.gelu(summed, approximate=False).astype(jnp.bfloat16)


def on_device(
    analysis,
    send_rows,
    send_count,
    corner_slot,
    corner_weight,
    beside,
    quarter_turns,
    kernel_one,
    kernel_two,
    kernel_three,
):
    shards = lax.axis_size("tile")
    groups = lax.axis_size("chan")
    tiles_here = corner_slot.shape[1]
    near_count = send_rows.shape[1]
    capacity = send_rows.shape[2]
    channels_here = analysis.shape[0]
    pixels = corner_slot.shape[2]
    total_tiles = tiles_here * shards
    per_group = tiles_here // groups
    widths = [kernel_one.shape[2], kernel_two.shape[2], kernel_three.shape[2]]
    joined_kernels = jnp.concatenate([kernel_one, kernel_two, kernel_three], axis=2)
    joined_kernels = gather_by_exchange(joined_kernels, "chan", 1)
    kernels = []
    low = 0
    for width in widths:
        kernels.append(joined_kernels[:, :, low : low + width])
        low += width
    slot_order = jnp.arange(capacity)
    rows_list = send_rows[0].reshape(-1)
    piece = jnp.take(analysis, rows_list, axis=1)
    is_live = (slot_order[None, :] < send_count[0][:, None]).reshape(-1)
    piece = jnp.where(is_live[None, :], piece, jnp.zeros((), piece.dtype))
    blocks = []
    for offset_index in range(near_count):
        block = piece[:, offset_index * capacity : (offset_index + 1) * capacity]
        if offset_index != REACH:
            block = from_behind(block, "tile", offset_index - REACH)
        blocks.append(block)
    arrived = jnp.concatenate(blocks, axis=1)
    arrived = gather_by_exchange(arrived, "chan", 0)
    group_index = lax.axis_index("chan")
    my_slots = lax.dynamic_slice_in_dim(corner_slot, group_index * per_group, per_group, 1)
    my_weights = lax.dynamic_slice_in_dim(corner_weight, group_index * per_group, per_group, 1)
    my_slots = my_slots.reshape(my_slots.shape[0], per_group * pixels)
    my_weights = my_weights.reshape(my_weights.shape[0], per_group * pixels)
    slot_ids = jnp.arange(near_count * capacity)
    summed = None
    for corner in range(my_slots.shape[0]):
        one_hot = (slot_ids[:, None] == my_slots[corner][None, :]).astype(arrived.dtype)
        picked = jnp.dot(arrived, one_hot, preferred_element_type=jnp.float32)
        term = picked * my_weights[corner][None, :]
        summed = term if summed is None else summed + term
    activity = summed.astype(jnp.bfloat16).reshape(arrived.shape[0], per_group, pixels)
    first_tile = lax.axis_index(("tile", "chan")) * per_group
    near_beside = lax.dynamic_slice_in_dim(beside, group_index * per_group, per_group, 0)
    near_turns = lax.dynamic_slice_in_dim(quarter_turns, group_index * per_group, per_group, 0)
    local_beside = jnp.remainder(near_beside - first_tile + REACH, total_tiles)

    def joined_rims(cycle_vals):
        return extended_2(cycle_vals, ((("tile", "chan"), 1),), REACH)

    where_from = padded_index(per_group, local_beside, near_turns)
    for kernel in kernels:
        activity = conv_layer(activity, kernel, where_from, joined_rims)
    result = lax.all_to_all(activity, "chan", split_axis=0, concat_axis=1, tiled=True)
    return result


def solution(mesh):
    step = jax.shard_map(
        on_device,
        mesh=mesh,
        in_specs=(
            P("chan", "tile"),
            P("tile", None, None),
            P("tile", None),
            P(None, "tile", None),
            P(None, "tile", None),
            P("tile", None),
            P("tile", None),
            P(None, "chan", None),
            P(None, "chan", None),
            P(None, "chan", None),
        ),
        out_specs=P("chan", "tile", None),
        check_vma=False,
    )
    return step
```

```python
import jax
import jax.numpy as jnp
import numpy as np
from jax import lax
from jax.sharding import PartitionSpec as P

P_SIZE = 16
REACH = 2


def from_behind(value, axis, steps):
    count = lax.axis_size(axis)
    pairs = [(source, (source + steps) % count) for source in range(count)]
    return lax.ppermute(value, axis, pairs)


def gather_by_exchange(value, axis, dim):
    count = lax.axis_size(axis)
    shape = value.shape
    copies = jnp.broadcast_to(
        jnp.expand_dims(value, dim), shape[:dim] + (count,) + shape[dim:]
    )
    copies = copies.reshape(shape[:dim] + (count * shape[dim],) + shape[dim + 1 :])
    return lax.all_to_all(copies, axis, split_axis=dim, concat_axis=dim, tiled=True)


def extended_2(x, sides, width):
    for axis, dim in sides:
        size, length = (lax.axis_size(axis), x.shape[dim])
        up = [(i, (i + 1) % size) for i in range(size)]
        down = [(j, i) for i, j in up]
        last = lax.slice_in_dim(x, length - width, length, axis=dim)
        initial = lax.slice_in_dim(x, 0, width, axis=dim)
        before = lax.ppermute(last, axis, up)
        after = lax.ppermute(initial, axis, down)
        x = jnp.concatenate([before, x, after], axis=dim)
    return x


def cycle_table(extent):
    length = 4 * extent - 4
    entries = []
    for cycle_pos in range(length):
        if cycle_pos < extent:
            row_at, col_at = (cycle_pos, 0)
        elif cycle_pos < 2 * extent - 1:
            row_at, col_at = (extent - 1, cycle_pos - extent + 1)
        elif cycle_pos < 3 * extent - 2:
            row_at, col_at = (3 * extent - 3 - cycle_pos, extent - 1)
        else:
            row_at, col_at = (0, 4 * extent - 4 - cycle_pos)
        entries.append(row_at * extent + col_at)
    return np.array(entries, np.int32)


def border_tables(extent):
    length = 4 * extent - 4
    heading = []
    anchor = []
    for col_at in range(extent):
        heading.append(0)
        anchor.append(extent - 1 + col_at)
    for col_at in range(extent):
        heading.append(1)
        anchor.append((length - col_at) % length)
    for row_at in range(extent):
        heading.append(2)
        anchor.append(3 * extent - 3 - row_at)
    for row_at in range(extent):
        heading.append(3)
        anchor.append(row_at)
    heading += [4, 5, 6, 7]
    anchor += [2 * extent - 2, extent - 1, 3 * extent - 3, 0]
    return (np.array(heading, np.int32), np.array(anchor, np.int32))


def layout_table(extent):
    padded_side = extent + 2
    interior = extent * extent
    entries = []
    for row_at in range(padded_side):
        for col_at in range(padded_side):
            if 1 <= row_at <= extent and 1 <= col_at <= extent:
                entries.append((row_at - 1) * extent + col_at - 1)
            elif row_at == 0 and 1 <= col_at <= extent:
                entries.append(interior + col_at - 1)
            elif row_at == padded_side - 1 and 1 <= col_at <= extent:
                entries.append(interior + extent + col_at - 1)
            elif col_at == 0 and 1 <= row_at <= extent:
                entries.append(interior + 2 * extent + row_at - 1)
            elif col_at == padded_side - 1 and 1 <= row_at <= extent:
                entries.append(interior + 3 * extent + row_at - 1)
            else:
                corner = (0 if row_at == 0 else 2) + (0 if col_at == 0 else 1)
                entries.append(interior + 4 * extent + corner)
    return np.array(entries, np.int32)


def padded_index(tiles, local_beside, local_turns):
    length = 4 * P_SIZE - 4
    interior = P_SIZE * P_SIZE
    heading, anchor = border_tables(P_SIZE)
    near_tile = jnp.take(local_beside, heading, axis=1)
    near_turn = jnp.take(local_turns, heading, axis=1)
    source = near_tile * length + jnp.remainder(anchor[None, :] - near_turn * (P_SIZE - 1), length)
    layout = layout_table(P_SIZE)
    tile_ids = jnp.arange(tiles)[:, None]
    from_interior = tile_ids * interior + jnp.minimum(layout, interior - 1)[None, :]
    border_at = np.maximum(layout - interior, 0)
    from_border = tiles * interior + jnp.take(source, border_at, axis=1)
    return jnp.where((layout < interior)[None, :], from_interior, from_border)


def conv_layer(activity, kernel, where_from, gather_rims):
    cycle_vals = jnp.take(activity, cycle_table(P_SIZE), axis=2)
    extended = gather_rims(cycle_vals)
    channels, tiles = activity.shape[0], activity.shape[1]
    joined = jnp.concatenate(
        [activity.reshape(channels, -1), extended.reshape(channels, -1)], axis=1
    )
    padded_side = P_SIZE + 2
    padded = jnp.take(joined, where_from.reshape(-1), axis=1)
    padded = padded.reshape(channels, tiles, padded_side, padded_side)
    taps = kernel.reshape(3, 3, kernel.shape[1], kernel.shape[2])
    summed = lax.conv_general_dilated(
        padded,
        taps,
        window_strides=(1, 1),
        padding="VALID",
        dimension_numbers=("CNHW", "HWOI", "CNHW"),
        preferred_element_type=jnp.float32,
    )
    summed = summed.reshape(summed.shape[0], tiles, P_SIZE * P_SIZE)
    return jax.nn.gelu(summed, approximate=False).astype(jnp.bfloat16)


def on_device(
    analysis,
    send_rows,
    send_count,
    corner_slot,
    corner_weight,
    beside,
    quarter_turns,
    kernel_one,
    kernel_two,
    kernel_three,
):
    shards = lax.axis_size("tile")
    groups = lax.axis_size("chan")
    tiles_here = corner_slot.shape[1]
    near_count = send_rows.shape[1]
    capacity = send_rows.shape[2]
    channels_here = analysis.shape[0]
    pixels = corner_slot.shape[2]
    total_tiles = tiles_here * shards
    per_group = tiles_here // groups
    widths = [kernel_one.shape[2], kernel_two.shape[2], kernel_three.shape[2]]
    joined_kernels = jnp.concatenate([kernel_one, kernel_two, kernel_three], axis=2)
    joined_kernels = gather_by_exchange(joined_kernels, "chan", 1)
    kernels = []
    low = 0
    for width in widths:
        kernels.append(joined_kernels[:, :, low : low + width])
        low += width
    slot_order = jnp.arange(capacity)
    rows_list = send_rows[0].reshape(-1)
    piece = jnp.take(analysis, rows_list, axis=1)
    is_live = (slot_order[None, :] < send_count[0][:, None]).reshape(-1)
    piece = jnp.where(is_live[None, :], piece, jnp.zeros((), piece.dtype))
    blocks = []
    for offset_index in range(near_count):
        block = piece[:, offset_index * capacity : (offset_index + 1) * capacity]
        if offset_index != REACH:
            block = from_behind(block, "tile", offset_index - REACH)
        blocks.append(block)
    arrived = jnp.concatenate(blocks, axis=1)
    arrived = gather_by_exchange(arrived, "chan", 0)
    group_index = lax.axis_index("chan")
    my_slots = lax.dynamic_slice_in_dim(corner_slot, group_index * per_group, per_group, 1)
    my_weights = lax.dynamic_slice_in_dim(corner_weight, group_index * per_group, per_group, 1)
    my_slots = my_slots.reshape(my_slots.shape[0], per_group * pixels)
    my_weights = my_weights.reshape(my_weights.shape[0], per_group * pixels)
    slot_ids = jnp.arange(near_count * capacity)
    summed = None
    for corner in range(my_slots.shape[0]):
        one_hot = (slot_ids[:, None] == my_slots[corner][None, :]).astype(arrived.dtype)
        picked = jnp.dot(arrived, one_hot, preferred_element_type=jnp.float32)
        term = picked * my_weights[corner][None, :]
        summed = term if summed is None else summed + term
    activity = summed.astype(jnp.bfloat16).reshape(arrived.shape[0], per_group, pixels)
    first_tile = lax.axis_index(("tile", "chan")) * per_group
    near_beside = lax.dynamic_slice_in_dim(beside, group_index * per_group, per_group, 0)
    near_turns = lax.dynamic_slice_in_dim(quarter_turns, group_index * per_group, per_group, 0)
    local_beside = jnp.remainder(near_beside - first_tile + REACH, total_tiles)

    def joined_rims(cycle_vals):
        return extended_2(cycle_vals, ((("tile", "chan"), 1),), REACH)

    where_from = padded_index(per_group, local_beside, near_turns)
    for kernel in kernels:
        activity = conv_layer(activity, kernel, where_from, joined_rims)
    result = lax.all_to_all(activity, "chan", split_axis=0, concat_axis=1, tiled=True)
    return result


def solution(mesh):
    step = jax.shard_map(
        on_device,
        mesh=mesh,
        in_specs=(
            P("chan", "tile"),
            P("tile", None, None),
            P("tile", None),
            P(None, "tile", None),
            P(None, "tile", None),
            P("tile", None),
            P("tile", None),
            P(None, "chan", None),
            P(None, "chan", None),
            P(None, "chan", None),
        ),
        out_specs=P("chan", "tile", None),
        check_vma=False,
    )
    return step
```

```python
import jax
import jax.numpy as jnp
import numpy as np
from jax import lax
from jax.sharding import PartitionSpec as P

P_SIZE = 16
REACH = 2


def from_behind(value, axis, steps):
    count = lax.axis_size(axis)
    pairs = [(source, (source + steps) % count) for source in range(count)]
    return lax.ppermute(value, axis, pairs)


def gather_by_exchange(value, axis, dim):
    count = lax.axis_size(axis)
    shape = value.shape
    copies = jnp.broadcast_to(
        jnp.expand_dims(value, dim), shape[:dim] + (count,) + shape[dim:]
    )
    copies = copies.reshape(shape[:dim] + (count * shape[dim],) + shape[dim + 1 :])
    return lax.all_to_all(copies, axis, split_axis=dim, concat_axis=dim, tiled=True)


def extended_2(x, sides, width):
    for axis, dim in sides:
        size, length = (lax.axis_size(axis), x.shape[dim])
        up = [(i, (i + 1) % size) for i in range(size)]
        down = [(j, i) for i, j in up]
        last = lax.slice_in_dim(x, length - width, length, axis=dim)
        initial = lax.slice_in_dim(x, 0, width, axis=dim)
        before = lax.ppermute(last, axis, up)
        after = lax.ppermute(initial, axis, down)
        x = jnp.concatenate([before, x, after], axis=dim)
    return x


def cycle_table(extent):
    length = 4 * extent - 4
    entries = []
    for cycle_pos in range(length):
        if cycle_pos < extent:
            row_at, col_at = (cycle_pos, 0)
        elif cycle_pos < 2 * extent - 1:
            row_at, col_at = (extent - 1, cycle_pos - extent + 1)
        elif cycle_pos < 3 * extent - 2:
            row_at, col_at = (3 * extent - 3 - cycle_pos, extent - 1)
        else:
            row_at, col_at = (0, 4 * extent - 4 - cycle_pos)
        entries.append(row_at * extent + col_at)
    return np.array(entries, np.int32)


def border_tables(extent):
    length = 4 * extent - 4
    heading = []
    anchor = []
    for col_at in range(extent):
        heading.append(0)
        anchor.append(extent - 1 + col_at)
    for col_at in range(extent):
        heading.append(1)
        anchor.append((length - col_at) % length)
    for row_at in range(extent):
        heading.append(2)
        anchor.append(3 * extent - 3 - row_at)
    for row_at in range(extent):
        heading.append(3)
        anchor.append(row_at)
    heading += [4, 5, 6, 7]
    anchor += [2 * extent - 2, extent - 1, 3 * extent - 3, 0]
    return (np.array(heading, np.int32), np.array(anchor, np.int32))


def layout_table(extent):
    padded_side = extent + 2
    interior = extent * extent
    entries = []
    for row_at in range(padded_side):
        for col_at in range(padded_side):
            if 1 <= row_at <= extent and 1 <= col_at <= extent:
                entries.append((row_at - 1) * extent + col_at - 1)
            elif row_at == 0 and 1 <= col_at <= extent:
                entries.append(interior + col_at - 1)
            elif row_at == padded_side - 1 and 1 <= col_at <= extent:
                entries.append(interior + extent + col_at - 1)
            elif col_at == 0 and 1 <= row_at <= extent:
                entries.append(interior + 2 * extent + row_at - 1)
            elif col_at == padded_side - 1 and 1 <= row_at <= extent:
                entries.append(interior + 3 * extent + row_at - 1)
            else:
                corner = (0 if row_at == 0 else 2) + (0 if col_at == 0 else 1)
                entries.append(interior + 4 * extent + corner)
    return np.array(entries, np.int32)


def border_source(local_beside, local_turns):
    length = 4 * P_SIZE - 4
    heading, anchor = border_tables(P_SIZE)
    near_tile = jnp.take(local_beside, heading, axis=1)
    near_turn = jnp.take(local_turns, heading, axis=1)
    return near_tile * length + jnp.remainder(anchor[None, :] - near_turn * (P_SIZE - 1), length)


def rim_line(kernel, values, tap_ids):
    total = None
    for shift, tap in enumerate(tap_ids):
        part = jnp.einsum(
            "oc,ctq->otq",
            kernel[tap],
            values[:, :, shift : shift + P_SIZE],
            preferred_element_type=jnp.float32,
        )
        total = part if total is None else total + part
    return total


def conv_layer(activity, cycle_vals, kernel, source, gather_rims):
    extended = gather_rims(cycle_vals)
    channels, tiles = activity.shape[0], activity.shape[1]
    square = activity.reshape(channels, tiles, P_SIZE, P_SIZE)
    padded = jnp.pad(square, ((0, 0), (0, 0), (1, 1), (1, 1)))
    taps = kernel.reshape(3, 3, kernel.shape[1], kernel.shape[2])
    summed = lax.conv_general_dilated(
        padded,
        taps,
        window_strides=(1, 1),
        padding="VALID",
        dimension_numbers=("CNHW", "HWOI", "CNHW"),
        preferred_element_type=jnp.float32,
    )
    border = jnp.take(extended.reshape(channels, -1), source.reshape(-1), axis=1)
    border = border.reshape(channels, tiles, 4 * P_SIZE + 4)
    side = P_SIZE
    rims = [border[:, :, k * side : (k + 1) * side] for k in range(4)]
    corners = [border[:, :, 4 * side + k : 4 * side + k + 1] for k in range(4)]
    blank = jnp.zeros((channels, tiles, 1), border.dtype)
    top_row = jnp.concatenate([corners[0], rims[0], corners[1]], axis=2)
    bottom_row = jnp.concatenate([corners[2], rims[1], corners[3]], axis=2)
    left_col = jnp.concatenate([blank, rims[2], blank], axis=2)
    right_col = jnp.concatenate([blank, rims[3], blank], axis=2)
    summed = summed.at[:, :, 0, :].add(rim_line(kernel, top_row, (0, 1, 2)))
    summed = summed.at[:, :, side - 1, :].add(rim_line(kernel, bottom_row, (6, 7, 8)))
    summed = summed.at[:, :, :, 0].add(rim_line(kernel, left_col, (0, 3, 6)))
    summed = summed.at[:, :, :, side - 1].add(rim_line(kernel, right_col, (2, 5, 8)))
    summed = summed.reshape(summed.shape[0], tiles, side * side)
    ring = jnp.take(summed, cycle_table(P_SIZE), axis=2)
    next_cycles = jax.nn.gelu(ring, approximate=False).astype(jnp.bfloat16)
    return jax.nn.gelu(summed, approximate=False).astype(jnp.bfloat16), next_cycles


def on_device(
    analysis,
    send_rows,
    send_count,
    corner_slot,
    corner_weight,
    beside,
    quarter_turns,
    kernel_one,
    kernel_two,
    kernel_three,
):
    shards = lax.axis_size("tile")
    groups = lax.axis_size("chan")
    tiles_here = corner_slot.shape[1]
    near_count = send_rows.shape[1]
    capacity = send_rows.shape[2]
    channels_here = analysis.shape[0]
    pixels = corner_slot.shape[2]
    total_tiles = tiles_here * shards
    per_group = tiles_here // groups
    widths = [kernel_one.shape[2], kernel_two.shape[2], kernel_three.shape[2]]
    joined_kernels = jnp.concatenate([kernel_one, kernel_two, kernel_three], axis=2)
    joined_kernels = gather_by_exchange(joined_kernels, "chan", 1)
    kernels = []
    low = 0
    for width in widths:
        kernels.append(joined_kernels[:, :, low : low + width])
        low += width
    slot_order = jnp.arange(capacity)
    rows_list = send_rows[0].reshape(-1)
    piece = jnp.take(analysis, rows_list, axis=1)
    is_live = (slot_order[None, :] < send_count[0][:, None]).reshape(-1)
    piece = jnp.where(is_live[None, :], piece, jnp.zeros((), piece.dtype))
    blocks = []
    for offset_index in range(near_count):
        block = piece[:, offset_index * capacity : (offset_index + 1) * capacity]
        if offset_index != REACH:
            block = from_behind(block, "tile", offset_index - REACH)
        blocks.append(block)
    arrived = jnp.concatenate(blocks, axis=1)
    arrived = gather_by_exchange(arrived, "chan", 0)
    group_index = lax.axis_index("chan")
    my_slots = lax.dynamic_slice_in_dim(corner_slot, group_index * per_group, per_group, 1)
    my_weights = lax.dynamic_slice_in_dim(corner_weight, group_index * per_group, per_group, 1)
    my_slots = my_slots.reshape(my_slots.shape[0], per_group * pixels)
    my_weights = my_weights.reshape(my_weights.shape[0], per_group * pixels)
    slot_ids = jnp.arange(near_count * capacity)
    summed = None
    for corner in range(my_slots.shape[0]):
        one_hot = (slot_ids[:, None] == my_slots[corner][None, :]).astype(arrived.dtype)
        picked = jnp.dot(arrived, one_hot, preferred_element_type=jnp.float32)
        term = picked * my_weights[corner][None, :]
        summed = term if summed is None else summed + term
    activity = summed.astype(jnp.bfloat16).reshape(arrived.shape[0], per_group, pixels)
    first_tile = lax.axis_index(("tile", "chan")) * per_group
    near_beside = lax.dynamic_slice_in_dim(beside, group_index * per_group, per_group, 0)
    near_turns = lax.dynamic_slice_in_dim(quarter_turns, group_index * per_group, per_group, 0)
    local_beside = jnp.remainder(near_beside - first_tile + REACH, total_tiles)

    def joined_rims(cycle_vals):
        return extended_2(cycle_vals, ((("tile", "chan"), 1),), REACH)

    source = border_source(local_beside, near_turns)
    cycle_vals = jnp.take(activity, cycle_table(P_SIZE), axis=2)
    for kernel in kernels:
        activity, cycle_vals = conv_layer(activity, cycle_vals, kernel, source, joined_rims)
    result = lax.all_to_all(activity, "chan", split_axis=0, concat_axis=1, tiled=True)
    return result


def solution(mesh):
    step = jax.shard_map(
        on_device,
        mesh=mesh,
        in_specs=(
            P("chan", "tile"),
            P("tile", None, None),
            P("tile", None),
            P(None, "tile", None),
            P(None, "tile", None),
            P("tile", None),
            P("tile", None),
            P(None, "chan", None),
            P(None, "chan", None),
            P(None, "chan", None),
        ),
        out_specs=P("chan", "tile", None),
        check_vma=False,
    )
    return step
```

```python
import jax
import jax.numpy as jnp
import numpy as np
from jax import lax
from jax.sharding import PartitionSpec as P

P_SIZE = 16
REACH = 2


def from_behind(value, axis, steps):
    count = lax.axis_size(axis)
    pairs = [(source, (source + steps) % count) for source in range(count)]
    return lax.ppermute(value, axis, pairs)


def gather_by_exchange(value, axis, dim):
    count = lax.axis_size(axis)
    shape = value.shape
    copies = jnp.broadcast_to(
        jnp.expand_dims(value, dim), shape[:dim] + (count,) + shape[dim:]
    )
    copies = copies.reshape(shape[:dim] + (count * shape[dim],) + shape[dim + 1 :])
    return lax.all_to_all(copies, axis, split_axis=dim, concat_axis=dim, tiled=True)


def extended_2(x, sides, width, hold):
    for axis, dim in sides:
        size, length = (lax.axis_size(axis), x.shape[dim])
        up = [(i, (i + 1) % size) for i in range(size)]
        down = [(j, i) for i, j in up]
        last = lax.slice_in_dim(x, length - width, length, axis=dim)
        initial = lax.slice_in_dim(x, 0, width, axis=dim)
        before = lax.ppermute(last, axis, up)
        initial, _ = lax.optimization_barrier((initial, hold))
        after = lax.ppermute(initial, axis, down)
        x = jnp.concatenate([before, x, after], axis=dim)
    return x


def cycle_table(extent):
    length = 4 * extent - 4
    entries = []
    for cycle_pos in range(length):
        if cycle_pos < extent:
            row_at, col_at = (cycle_pos, 0)
        elif cycle_pos < 2 * extent - 1:
            row_at, col_at = (extent - 1, cycle_pos - extent + 1)
        elif cycle_pos < 3 * extent - 2:
            row_at, col_at = (3 * extent - 3 - cycle_pos, extent - 1)
        else:
            row_at, col_at = (0, 4 * extent - 4 - cycle_pos)
        entries.append(row_at * extent + col_at)
    return np.array(entries, np.int32)


def border_tables(extent):
    length = 4 * extent - 4
    heading = []
    anchor = []
    for col_at in range(extent):
        heading.append(0)
        anchor.append(extent - 1 + col_at)
    for col_at in range(extent):
        heading.append(1)
        anchor.append((length - col_at) % length)
    for row_at in range(extent):
        heading.append(2)
        anchor.append(3 * extent - 3 - row_at)
    for row_at in range(extent):
        heading.append(3)
        anchor.append(row_at)
    heading += [4, 5, 6, 7]
    anchor += [2 * extent - 2, extent - 1, 3 * extent - 3, 0]
    return (np.array(heading, np.int32), np.array(anchor, np.int32))


def layout_table(extent):
    padded_side = extent + 2
    interior = extent * extent
    entries = []
    for row_at in range(padded_side):
        for col_at in range(padded_side):
            if 1 <= row_at <= extent and 1 <= col_at <= extent:
                entries.append((row_at - 1) * extent + col_at - 1)
            elif row_at == 0 and 1 <= col_at <= extent:
                entries.append(interior + col_at - 1)
            elif row_at == padded_side - 1 and 1 <= col_at <= extent:
                entries.append(interior + extent + col_at - 1)
            elif col_at == 0 and 1 <= row_at <= extent:
                entries.append(interior + 2 * extent + row_at - 1)
            elif col_at == padded_side - 1 and 1 <= row_at <= extent:
                entries.append(interior + 3 * extent + row_at - 1)
            else:
                corner = (0 if row_at == 0 else 2) + (0 if col_at == 0 else 1)
                entries.append(interior + 4 * extent + corner)
    return np.array(entries, np.int32)


def border_source(local_beside, local_turns):
    length = 4 * P_SIZE - 4
    heading, anchor = border_tables(P_SIZE)
    near_tile = jnp.take(local_beside, heading, axis=1)
    near_turn = jnp.take(local_turns, heading, axis=1)
    return near_tile * length + jnp.remainder(anchor[None, :] - near_turn * (P_SIZE - 1), length)


def rim_line(kernel, values, tap_ids):
    total = None
    for shift, tap in enumerate(tap_ids):
        part = jnp.einsum(
            "oc,ctq->otq",
            kernel[tap],
            values[:, :, shift : shift + P_SIZE],
            preferred_element_type=jnp.float32,
        )
        total = part if total is None else total + part
    return total


def conv_layer(activity, cycle_vals, kernel, source, gather_rims):
    channels, tiles = activity.shape[0], activity.shape[1]
    square = activity.reshape(channels, tiles, P_SIZE, P_SIZE)
    padded = jnp.pad(square, ((0, 0), (0, 0), (1, 1), (1, 1)))
    taps = kernel.reshape(3, 3, kernel.shape[1], kernel.shape[2])
    summed = lax.conv_general_dilated(
        padded,
        taps,
        window_strides=(1, 1),
        padding="VALID",
        dimension_numbers=("CNHW", "HWOI", "CNHW"),
        preferred_element_type=jnp.float32,
    )
    extended = gather_rims(cycle_vals, summed)
    border = jnp.take(extended.reshape(channels, -1), source.reshape(-1), axis=1)
    border = border.reshape(channels, tiles, 4 * P_SIZE + 4)
    side = P_SIZE
    rims = [border[:, :, k * side : (k + 1) * side] for k in range(4)]
    corners = [border[:, :, 4 * side + k : 4 * side + k + 1] for k in range(4)]
    blank = jnp.zeros((channels, tiles, 1), border.dtype)
    top_row = jnp.concatenate([corners[0], rims[0], corners[1]], axis=2)
    bottom_row = jnp.concatenate([corners[2], rims[1], corners[3]], axis=2)
    left_col = jnp.concatenate([blank, rims[2], blank], axis=2)
    right_col = jnp.concatenate([blank, rims[3], blank], axis=2)
    summed = summed.at[:, :, 0, :].add(rim_line(kernel, top_row, (0, 1, 2)))
    summed = summed.at[:, :, side - 1, :].add(rim_line(kernel, bottom_row, (6, 7, 8)))
    summed = summed.at[:, :, :, 0].add(rim_line(kernel, left_col, (0, 3, 6)))
    summed = summed.at[:, :, :, side - 1].add(rim_line(kernel, right_col, (2, 5, 8)))
    summed = summed.reshape(summed.shape[0], tiles, side * side)
    ring = jnp.take(summed, cycle_table(P_SIZE), axis=2)
    next_cycles = jax.nn.gelu(ring, approximate=False).astype(jnp.bfloat16)
    return jax.nn.gelu(summed, approximate=False).astype(jnp.bfloat16), next_cycles


def on_device(
    analysis,
    send_rows,
    send_count,
    corner_slot,
    corner_weight,
    beside,
    quarter_turns,
    kernel_one,
    kernel_two,
    kernel_three,
):
    shards = lax.axis_size("tile")
    groups = lax.axis_size("chan")
    tiles_here = corner_slot.shape[1]
    near_count = send_rows.shape[1]
    capacity = send_rows.shape[2]
    channels_here = analysis.shape[0]
    pixels = corner_slot.shape[2]
    total_tiles = tiles_here * shards
    per_group = tiles_here // groups
    widths = [kernel_one.shape[2], kernel_two.shape[2], kernel_three.shape[2]]
    joined_kernels = jnp.concatenate([kernel_one, kernel_two, kernel_three], axis=2)
    joined_kernels = gather_by_exchange(joined_kernels, "chan", 1)
    kernels = []
    low = 0
    for width in widths:
        kernels.append(joined_kernels[:, :, low : low + width])
        low += width
    slot_order = jnp.arange(capacity)
    rows_list = send_rows[0].reshape(-1)
    piece = jnp.take(analysis, rows_list, axis=1)
    is_live = (slot_order[None, :] < send_count[0][:, None]).reshape(-1)
    piece = jnp.where(is_live[None, :], piece, jnp.zeros((), piece.dtype))
    blocks = []
    for offset_index in range(near_count):
        block = piece[:, offset_index * capacity : (offset_index + 1) * capacity]
        if offset_index != REACH:
            block = from_behind(block, "tile", offset_index - REACH)
        blocks.append(block)
    arrived = jnp.concatenate(blocks, axis=1)
    arrived = gather_by_exchange(arrived, "chan", 0)
    group_index = lax.axis_index("chan")
    my_slots = lax.dynamic_slice_in_dim(corner_slot, group_index * per_group, per_group, 1)
    my_weights = lax.dynamic_slice_in_dim(corner_weight, group_index * per_group, per_group, 1)
    my_slots = my_slots.reshape(my_slots.shape[0], per_group * pixels)
    my_weights = my_weights.reshape(my_weights.shape[0], per_group * pixels)
    slot_ids = jnp.arange(near_count * capacity)
    summed = None
    for corner in range(my_slots.shape[0]):
        one_hot = (slot_ids[:, None] == my_slots[corner][None, :]).astype(arrived.dtype)
        picked = jnp.dot(arrived, one_hot, preferred_element_type=jnp.float32)
        term = picked * my_weights[corner][None, :]
        summed = term if summed is None else summed + term
    activity = summed.astype(jnp.bfloat16).reshape(arrived.shape[0], per_group, pixels)
    first_tile = lax.axis_index(("tile", "chan")) * per_group
    near_beside = lax.dynamic_slice_in_dim(beside, group_index * per_group, per_group, 0)
    near_turns = lax.dynamic_slice_in_dim(quarter_turns, group_index * per_group, per_group, 0)
    local_beside = jnp.remainder(near_beside - first_tile + REACH, total_tiles)

    def joined_rims(cycle_vals, hold):
        return extended_2(cycle_vals, ((("tile", "chan"), 1),), REACH, hold)

    source = border_source(local_beside, near_turns)
    cycle_vals = jnp.take(activity, cycle_table(P_SIZE), axis=2)
    for kernel in kernels:
        activity, cycle_vals = conv_layer(activity, cycle_vals, kernel, source, joined_rims)
    result = lax.all_to_all(activity, "chan", split_axis=0, concat_axis=1, tiled=True)
    return result


def solution(mesh):
    step = jax.shard_map(
        on_device,
        mesh=mesh,
        in_specs=(
            P("chan", "tile"),
            P("tile", None, None),
            P("tile", None),
            P(None, "tile", None),
            P(None, "tile", None),
            P("tile", None),
            P("tile", None),
            P(None, "chan", None),
            P(None, "chan", None),
            P(None, "chan", None),
        ),
        out_specs=P("chan", "tile", None),
        check_vma=False,
    )
    return step
```

```python
import jax
import jax.numpy as jnp
import numpy as np
from jax import lax
from jax.sharding import PartitionSpec as P

P_SIZE = 16
REACH = 2


def from_behind(value, axis, steps):
    count = lax.axis_size(axis)
    pairs = [(source, (source + steps) % count) for source in range(count)]
    return lax.ppermute(value, axis, pairs)


def gather_by_exchange(value, axis, dim):
    count = lax.axis_size(axis)
    shape = value.shape
    copies = jnp.broadcast_to(
        jnp.expand_dims(value, dim), shape[:dim] + (count,) + shape[dim:]
    )
    copies = copies.reshape(shape[:dim] + (count * shape[dim],) + shape[dim + 1 :])
    return lax.all_to_all(copies, axis, split_axis=dim, concat_axis=dim, tiled=True)


def extended_2(x, sides, width):
    for axis, dim in sides:
        size, length = (lax.axis_size(axis), x.shape[dim])
        up = [(i, (i + 1) % size) for i in range(size)]
        down = [(j, i) for i, j in up]
        last = lax.slice_in_dim(x, length - width, length, axis=dim)
        initial = lax.slice_in_dim(x, 0, width, axis=dim)
        before = lax.ppermute(last, axis, up)
        after = lax.ppermute(initial, axis, down)
        x = jnp.concatenate([before, x, after], axis=dim)
    return x


def cycle_table(extent):
    length = 4 * extent - 4
    entries = []
    for cycle_pos in range(length):
        if cycle_pos < extent:
            row_at, col_at = (cycle_pos, 0)
        elif cycle_pos < 2 * extent - 1:
            row_at, col_at = (extent - 1, cycle_pos - extent + 1)
        elif cycle_pos < 3 * extent - 2:
            row_at, col_at = (3 * extent - 3 - cycle_pos, extent - 1)
        else:
            row_at, col_at = (0, 4 * extent - 4 - cycle_pos)
        entries.append(row_at * extent + col_at)
    return np.array(entries, np.int32)


def border_tables(extent):
    length = 4 * extent - 4
    heading = []
    anchor = []
    for col_at in range(extent):
        heading.append(0)
        anchor.append(extent - 1 + col_at)
    for col_at in range(extent):
        heading.append(1)
        anchor.append((length - col_at) % length)
    for row_at in range(extent):
        heading.append(2)
        anchor.append(3 * extent - 3 - row_at)
    for row_at in range(extent):
        heading.append(3)
        anchor.append(row_at)
    heading += [4, 5, 6, 7]
    anchor += [2 * extent - 2, extent - 1, 3 * extent - 3, 0]
    return (np.array(heading, np.int32), np.array(anchor, np.int32))


def border_source(local_beside, local_turns):
    length = 4 * P_SIZE - 4
    heading, anchor = border_tables(P_SIZE)
    near_tile = jnp.take(local_beside, heading, axis=1)
    near_turn = jnp.take(local_turns, heading, axis=1)
    return near_tile * length + jnp.remainder(anchor[None, :] - near_turn * (P_SIZE - 1), length)


def rim_line(kernel, values, tap_ids):
    total = None
    for shift, tap in enumerate(tap_ids):
        part = jnp.einsum(
            "oc,ctq->otq",
            kernel[tap],
            values[:, :, shift : shift + P_SIZE],
            preferred_element_type=jnp.float32,
        )
        total = part if total is None else total + part
    return total


def conv_layer(activity, cycle_vals, kernel, source, gather_rims):
    extended = gather_rims(cycle_vals)
    channels, tiles = activity.shape[0], activity.shape[1]
    square = activity.reshape(channels, tiles, P_SIZE, P_SIZE)
    padded = jnp.pad(square, ((0, 0), (0, 0), (1, 1), (1, 1)))
    taps = kernel.reshape(3, 3, kernel.shape[1], kernel.shape[2])
    summed = lax.conv_general_dilated(
        padded,
        taps,
        window_strides=(1, 1),
        padding="VALID",
        dimension_numbers=("CNHW", "HWOI", "CNHW"),
        preferred_element_type=jnp.float32,
    )
    border = jnp.take(extended.reshape(channels, -1), source.reshape(-1), axis=1)
    border = border.reshape(channels, tiles, 4 * P_SIZE + 4)
    side = P_SIZE
    rims = [border[:, :, k * side : (k + 1) * side] for k in range(4)]
    corners = [border[:, :, 4 * side + k : 4 * side + k + 1] for k in range(4)]
    blank = jnp.zeros((channels, tiles, 1), border.dtype)
    top_row = jnp.concatenate([corners[0], rims[0], corners[1]], axis=2)
    bottom_row = jnp.concatenate([corners[2], rims[1], corners[3]], axis=2)
    left_col = jnp.concatenate([blank, rims[2], blank], axis=2)
    right_col = jnp.concatenate([blank, rims[3], blank], axis=2)
    summed = summed.at[:, :, 0, :].add(rim_line(kernel, top_row, (0, 1, 2)))
    summed = summed.at[:, :, side - 1, :].add(rim_line(kernel, bottom_row, (6, 7, 8)))
    summed = summed.at[:, :, :, 0].add(rim_line(kernel, left_col, (0, 3, 6)))
    summed = summed.at[:, :, :, side - 1].add(rim_line(kernel, right_col, (2, 5, 8)))
    summed = summed.reshape(summed.shape[0], tiles, side * side)
    ring = jnp.take(summed, cycle_table(P_SIZE), axis=2)
    next_cycles = jax.nn.gelu(ring, approximate=False).astype(jnp.bfloat16)
    full = jax.nn.gelu(summed, approximate=False).astype(jnp.bfloat16)
    return full, next_cycles


def on_device(
    analysis,
    send_rows,
    send_count,
    corner_slot,
    corner_weight,
    beside,
    quarter_turns,
    kernel_one,
    kernel_two,
    kernel_three,
):
    shards = lax.axis_size("tile")
    groups = lax.axis_size("chan")
    tiles_here = corner_slot.shape[1]
    near_count = send_rows.shape[1]
    capacity = send_rows.shape[2]
    pixels = corner_slot.shape[2]
    total_tiles = tiles_here * shards
    per_group = tiles_here // groups
    widths = [kernel_one.shape[2], kernel_two.shape[2], kernel_three.shape[2]]
    joined_kernels = jnp.concatenate([kernel_one, kernel_two, kernel_three], axis=2)
    joined_kernels = gather_by_exchange(joined_kernels, "chan", 1)
    kernels = []
    low = 0
    for width in widths:
        kernels.append(joined_kernels[:, :, low : low + width])
        low += width
    slot_order = jnp.arange(capacity)
    rows_list = send_rows[0].reshape(-1)
    piece = jnp.take(analysis, rows_list, axis=1)
    is_live = (slot_order[None, :] < send_count[0][:, None]).reshape(-1)
    piece = jnp.where(is_live[None, :], piece, jnp.zeros((), piece.dtype))
    blocks = []
    for offset_index in range(near_count):
        block = piece[:, offset_index * capacity : (offset_index + 1) * capacity]
        if offset_index != REACH:
            block = from_behind(block, "tile", offset_index - REACH)
        blocks.append(block)
    arrived = jnp.concatenate(blocks, axis=1)
    arrived = gather_by_exchange(arrived, "chan", 0)
    group_index = lax.axis_index("chan")
    my_slots = lax.dynamic_slice_in_dim(corner_slot, group_index * per_group, per_group, 1)
    my_weights = lax.dynamic_slice_in_dim(corner_weight, group_index * per_group, per_group, 1)
    my_slots = my_slots.reshape(my_slots.shape[0], per_group * pixels)
    my_weights = my_weights.reshape(my_weights.shape[0], per_group * pixels)
    slot_ids = jnp.arange(near_count * capacity)
    summed = None
    for corner in range(my_slots.shape[0]):
        one_hot = (slot_ids[:, None] == my_slots[corner][None, :]).astype(arrived.dtype)
        picked = jnp.dot(arrived, one_hot, preferred_element_type=jnp.float32)
        term = picked * my_weights[corner][None, :]
        summed = term if summed is None else summed + term
    activity = summed.astype(jnp.bfloat16).reshape(arrived.shape[0], per_group, pixels)
    first_tile = lax.axis_index(("tile", "chan")) * per_group
    near_beside = lax.dynamic_slice_in_dim(beside, group_index * per_group, per_group, 0)
    near_turns = lax.dynamic_slice_in_dim(quarter_turns, group_index * per_group, per_group, 0)
    local_beside = jnp.remainder(near_beside - first_tile + REACH, total_tiles)

    def joined_rims(cycle_vals):
        return extended_2(cycle_vals, ((("tile", "chan"), 1),), REACH)

    source = border_source(local_beside, near_turns)
    cycle_vals = jnp.take(activity, cycle_table(P_SIZE), axis=2)
    for kernel in kernels:
        activity, cycle_vals = conv_layer(activity, cycle_vals, kernel, source, joined_rims)
    result = lax.all_to_all(activity, "chan", split_axis=0, concat_axis=1, tiled=True)
    return result


def solution(mesh):
    return jax.shard_map(
        on_device,
        mesh=mesh,
        in_specs=(
            P("chan", "tile"),
            P("tile", None, None),
            P("tile", None),
            P(None, "tile", None),
            P(None, "tile", None),
            P("tile", None),
            P("tile", None),
            P(None, "chan", None),
            P(None, "chan", None),
            P(None, "chan", None),
        ),
        out_specs=P("chan", "tile", None),
        check_vma=False,
    )
```

```python
import jax
import jax.numpy as jnp
import numpy as np
from jax import lax
from jax.sharding import PartitionSpec as P

P_SIZE = 16
REACH = 2


def from_behind(value, axis, steps):
    count = lax.axis_size(axis)
    pairs = [(source, (source + steps) % count) for source in range(count)]
    return lax.ppermute(value, axis, pairs)


def gather_by_exchange(value, axis, dim):
    count = lax.axis_size(axis)
    shape = value.shape
    copies = jnp.broadcast_to(
        jnp.expand_dims(value, dim), shape[:dim] + (count,) + shape[dim:]
    )
    copies = copies.reshape(shape[:dim] + (count * shape[dim],) + shape[dim + 1 :])
    return lax.all_to_all(copies, axis, split_axis=dim, concat_axis=dim, tiled=True)


def extended_2(x, sides, width):
    for axis, dim in sides:
        size, length = (lax.axis_size(axis), x.shape[dim])
        up = [(i, (i + 1) % size) for i in range(size)]
        down = [(j, i) for i, j in up]
        last = lax.slice_in_dim(x, length - width, length, axis=dim)
        initial = lax.slice_in_dim(x, 0, width, axis=dim)
        before = lax.ppermute(last, axis, up)
        after = lax.ppermute(initial, axis, down)
        x = jnp.concatenate([before, x, after], axis=dim)
    return x


def cycle_table(extent):
    length = 4 * extent - 4
    entries = []
    for cycle_pos in range(length):
        if cycle_pos < extent:
            row_at, col_at = (cycle_pos, 0)
        elif cycle_pos < 2 * extent - 1:
            row_at, col_at = (extent - 1, cycle_pos - extent + 1)
        elif cycle_pos < 3 * extent - 2:
            row_at, col_at = (3 * extent - 3 - cycle_pos, extent - 1)
        else:
            row_at, col_at = (0, 4 * extent - 4 - cycle_pos)
        entries.append(row_at * extent + col_at)
    return np.array(entries, np.int32)


def border_tables(extent):
    length = 4 * extent - 4
    heading = []
    anchor = []
    for col_at in range(extent):
        heading.append(0)
        anchor.append(extent - 1 + col_at)
    for col_at in range(extent):
        heading.append(1)
        anchor.append((length - col_at) % length)
    for row_at in range(extent):
        heading.append(2)
        anchor.append(3 * extent - 3 - row_at)
    for row_at in range(extent):
        heading.append(3)
        anchor.append(row_at)
    heading += [4, 5, 6, 7]
    anchor += [2 * extent - 2, extent - 1, 3 * extent - 3, 0]
    return (np.array(heading, np.int32), np.array(anchor, np.int32))


def layout_table(extent):
    padded_side = extent + 2
    interior = extent * extent
    entries = []
    for row_at in range(padded_side):
        for col_at in range(padded_side):
            if 1 <= row_at <= extent and 1 <= col_at <= extent:
                entries.append((row_at - 1) * extent + col_at - 1)
            elif row_at == 0 and 1 <= col_at <= extent:
                entries.append(interior + col_at - 1)
            elif row_at == padded_side - 1 and 1 <= col_at <= extent:
                entries.append(interior + extent + col_at - 1)
            elif col_at == 0 and 1 <= row_at <= extent:
                entries.append(interior + 2 * extent + row_at - 1)
            elif col_at == padded_side - 1 and 1 <= row_at <= extent:
                entries.append(interior + 3 * extent + row_at - 1)
            else:
                corner = (0 if row_at == 0 else 2) + (0 if col_at == 0 else 1)
                entries.append(interior + 4 * extent + corner)
    return np.array(entries, np.int32)


def border_source(local_beside, local_turns):
    length = 4 * P_SIZE - 4
    heading, anchor = border_tables(P_SIZE)
    near_tile = jnp.take(local_beside, heading, axis=1)
    near_turn = jnp.take(local_turns, heading, axis=1)
    return near_tile * length + jnp.remainder(anchor[None, :] - near_turn * (P_SIZE - 1), length)


def rim_line(kernel, values, tap_ids):
    total = None
    for shift, tap in enumerate(tap_ids):
        part = jnp.einsum(
            "oc,ctq->otq",
            kernel[tap],
            values[:, :, shift : shift + P_SIZE],
            preferred_element_type=jnp.float32,
        )
        total = part if total is None else total + part
    return total


def conv_layer(activity, cycle_vals, kernel, source, gather_rims):
    extended = gather_rims(cycle_vals)
    channels, tiles = activity.shape[0], activity.shape[1]
    square = activity.reshape(channels, tiles, P_SIZE, P_SIZE)
    padded = jnp.pad(square, ((0, 0), (0, 0), (1, 1), (1, 1)))
    taps = kernel.reshape(3, 3, kernel.shape[1], kernel.shape[2])
    summed = lax.conv_general_dilated(
        padded,
        taps,
        window_strides=(1, 1),
        padding="VALID",
        dimension_numbers=("CNHW", "HWOI", "CNHW"),
        preferred_element_type=jnp.float32,
    )
    border = jnp.take(extended.reshape(channels, -1), source.reshape(-1), axis=1)
    border = border.reshape(channels, tiles, 4 * P_SIZE + 4)
    side = P_SIZE
    rims = [border[:, :, k * side : (k + 1) * side] for k in range(4)]
    corners = [border[:, :, 4 * side + k : 4 * side + k + 1] for k in range(4)]
    blank = jnp.zeros((channels, tiles, 1), border.dtype)
    top_row = jnp.concatenate([corners[0], rims[0], corners[1]], axis=2)
    bottom_row = jnp.concatenate([corners[2], rims[1], corners[3]], axis=2)
    left_col = jnp.concatenate([blank, rims[2], blank], axis=2)
    right_col = jnp.concatenate([blank, rims[3], blank], axis=2)
    lines = jnp.stack([top_row, bottom_row, left_col, right_col])
    windows = jnp.stack([lines[..., k : k + side] for k in range(3)], axis=1)
    line_taps = kernel[np.array([[0, 1, 2], [6, 7, 8], [0, 3, 6], [2, 5, 8]])]
    fixes = jnp.einsum(
        "lkoc,lkctq->lotq", line_taps, windows, preferred_element_type=jnp.float32
    )
    summed = summed.at[:, :, 0, :].add(fixes[0])
    summed = summed.at[:, :, side - 1, :].add(fixes[1])
    summed = summed.at[:, :, :, 0].add(fixes[2])
    summed = summed.at[:, :, :, side - 1].add(fixes[3])
    summed = summed.reshape(summed.shape[0], tiles, side * side)
    ring = jnp.take(summed, cycle_table(P_SIZE), axis=2)
    next_cycles = jax.nn.gelu(ring, approximate=False).astype(jnp.bfloat16)
    return jax.nn.gelu(summed, approximate=False).astype(jnp.bfloat16), next_cycles


def on_device(
    analysis,
    send_rows,
    send_count,
    corner_slot,
    corner_weight,
    beside,
    quarter_turns,
    kernel_one,
    kernel_two,
    kernel_three,
):
    shards = lax.axis_size("tile")
    groups = lax.axis_size("chan")
    tiles_here = corner_slot.shape[1]
    near_count = send_rows.shape[1]
    capacity = send_rows.shape[2]
    channels_here = analysis.shape[0]
    pixels = corner_slot.shape[2]
    total_tiles = tiles_here * shards
    per_group = tiles_here // groups
    widths = [kernel_one.shape[2], kernel_two.shape[2], kernel_three.shape[2]]
    joined_kernels = jnp.concatenate([kernel_one, kernel_two, kernel_three], axis=2)
    joined_kernels = gather_by_exchange(joined_kernels, "chan", 1)
    kernels = []
    low = 0
    for width in widths:
        kernels.append(joined_kernels[:, :, low : low + width])
        low += width
    slot_order = jnp.arange(capacity)
    rows_list = send_rows[0].reshape(-1)
    piece = jnp.take(analysis, rows_list, axis=1)
    is_live = (slot_order[None, :] < send_count[0][:, None]).reshape(-1)
    piece = jnp.where(is_live[None, :], piece, jnp.zeros((), piece.dtype))
    blocks = []
    for offset_index in range(near_count):
        block = piece[:, offset_index * capacity : (offset_index + 1) * capacity]
        if offset_index != REACH:
            block = from_behind(block, "tile", offset_index - REACH)
        blocks.append(block)
    arrived = jnp.concatenate(blocks, axis=1)
    arrived = gather_by_exchange(arrived, "chan", 0)
    group_index = lax.axis_index("chan")
    my_slots = lax.dynamic_slice_in_dim(corner_slot, group_index * per_group, per_group, 1)
    my_weights = lax.dynamic_slice_in_dim(corner_weight, group_index * per_group, per_group, 1)
    my_slots = my_slots.reshape(my_slots.shape[0], per_group * pixels)
    my_weights = my_weights.reshape(my_weights.shape[0], per_group * pixels)
    slot_ids = jnp.arange(near_count * capacity)
    summed = None
    for corner in range(my_slots.shape[0]):
        one_hot = (slot_ids[:, None] == my_slots[corner][None, :]).astype(arrived.dtype)
        picked = jnp.dot(arrived, one_hot, preferred_element_type=jnp.float32)
        term = picked * my_weights[corner][None, :]
        summed = term if summed is None else summed + term
    activity = summed.astype(jnp.bfloat16).reshape(arrived.shape[0], per_group, pixels)
    first_tile = lax.axis_index(("tile", "chan")) * per_group
    near_beside = lax.dynamic_slice_in_dim(beside, group_index * per_group, per_group, 0)
    near_turns = lax.dynamic_slice_in_dim(quarter_turns, group_index * per_group, per_group, 0)
    local_beside = jnp.remainder(near_beside - first_tile + REACH, total_tiles)

    def joined_rims(cycle_vals):
        return extended_2(cycle_vals, ((("tile", "chan"), 1),), REACH)

    source = border_source(local_beside, near_turns)
    cycle_vals = jnp.take(activity, cycle_table(P_SIZE), axis=2)
    for kernel in kernels:
        activity, cycle_vals = conv_layer(activity, cycle_vals, kernel, source, joined_rims)
    result = lax.all_to_all(activity, "chan", split_axis=0, concat_axis=1, tiled=True)
    return result


def solution(mesh):
    step = jax.shard_map(
        on_device,
        mesh=mesh,
        in_specs=(
            P("chan", "tile"),
            P("tile", None, None),
            P("tile", None),
            P(None, "tile", None),
            P(None, "tile", None),
            P("tile", None),
            P("tile", None),
            P(None, "chan", None),
            P(None, "chan", None),
            P(None, "chan", None),
        ),
        out_specs=P("chan", "tile", None),
        check_vma=False,
    )
    return step
```
